256 devices in a mesh: tm: 16 (over x, z_hi), dp: 16 (over y, z_lo, core).
Axes of the slice: x: 4, y: 4, z: 8 (z_hi: 4, z_lo: 2; z = z_hi * 2 + z_lo), core: 2. Of those that a mesh axis runs over, the one named last changes fastest.
Arguments:
- query_raw: bfloat16 [16, 2048, 1536], P('dp', 'tm'), may hold values from -60 to 60
- key_raw: bfloat16 [16, 2048, 1536], P('dp', 'tm'), may hold values from -60 to 60
- value_rows: bfloat16 [16, 2048, 1536], P('dp', 'tm'), may hold values from -6 to 6
- out_grad: bfloat16 [16, 2048, 1536], P('dp', 'tm'), may hold values from -6 to 6
- query_gain: float32 [128], replicated, may hold values from 0.5 to 9
- key_gain: float32 [128], replicated, may hold values from 0.5 to 9
- block_mask: int32 [16, 16, 4, 4], replicated, may hold values from 0 to 1, as said below
Outputs:
- attn_out: bfloat16 [16, 2048, 1536], P('dp', 'tm')
- query_grad: bfloat16 [16, 2048, 1536], P('dp', 'tm')
- key_grad: bfloat16 [16, 2048, 1536], P('dp', 'tm')
- value_grad: bfloat16 [16, 2048, 1536], P('dp', 'tm')
- query_gain_grad: float32 [128], replicated
- key_gain_grad: float32 [128], replicated
The draws below stay inside these ranges and needn't reach their ends.
Inputs may be any that keep to these rules, and one draw needn't show every extreme that they name: block_mask[f, f] is all ones; block_mask[f, g] is all zeros unless |f - g| is a power of two.
All inputs are finite; a program needn't handle non-finite values.
Results may differ from the reference program's by a relative error of at most 0.025.
The reference program's roundings to bfloat16 on the way count: a program that leaves them out, or rounds other values in their place, can miss the bound.
Values may be sent and summed in bfloat16 or wider, within the bound.
No kernel may reach another device: no remote copies, remote signals or barrier semaphores. Data moves between devices by JAX's collectives and lax.ppermute only.
A program may use at most 128 MiB of HBM per device.

```python
import functools
import math
import jax
import jax.numpy as jnp
from jax import lax

HEADS = 12
HEAD_DIM = 128
FRAME_TOK = 128
BLK = 32
NB = 4
FRAMES = 16
LEVELS = 4
CLIPS = 16
TOKENS = 2048
WIDTH = 1536


def query_key_pair(key):
    base = jax.random.fold_in(key, 71)
    first, second, third, fourth = jax.random.split(base, 4)
    shape = (CLIPS, TOKENS, HEADS, HEAD_DIM)
    query = jnp.clip(jax.random.normal(first, shape, jnp.float32), -5.0, 5.0)
    keys = jnp.clip(jax.random.normal(second, shape, jnp.float32), -5.0, 5.0)
    query = query * jnp.exp(jax.random.uniform(third, (CLIPS, TOKENS, HEADS, 1), jnp.float32, 0.0, math.log(10.0)))
    keys = keys * jnp.exp(jax.random.uniform(fourth, (CLIPS, TOKENS, HEADS, 1), jnp.float32, 0.0, math.log(10.0)))
    query = jnp.clip(query, -60.0, 60.0).reshape(CLIPS, TOKENS, HEADS * HEAD_DIM)
    keys = jnp.clip(keys, -60.0, 60.0).reshape(CLIPS, TOKENS, HEADS * HEAD_DIM)
    return (query, keys)


def draw_query_raw(key, part):
    return query_key_pair(key)[0].astype(jnp.bfloat16)


def draw_key_raw(key, part):
    return query_key_pair(key)[1].astype(jnp.bfloat16)


def gain_draw(key):
    return jnp.exp(jax.random.uniform(key, (HEAD_DIM,), jnp.float32, math.log(0.5), math.log(2.0)))


def draw_query_gain(key, part):
    return gain_draw(jax.random.fold_in(key, 5))


def draw_key_gain(key, part):
    return gain_draw(jax.random.fold_in(key, 6))


def draw_block_mask(key, part):
    first, second = jax.random.split(jax.random.fold_in(key, 9), 2)
    frames = jnp.arange(FRAMES, dtype=jnp.int32)
    gap = jnp.abs(frames[:, None] - frames[None, :])
    power = (gap > 0) & (gap & gap - 1 == 0)
    blocks = jnp.arange(NB, dtype=jnp.int32)
    band = jnp.abs(blocks[:, None] - blocks[None, :])
    inband = band[None, None] * gap[:, :, None, None] < NB
    extra = jax.random.randint(first, (FRAMES, FRAMES, NB, NB), 0, 4) == 0
    kept_pair = jax.random.randint(second, (FRAMES, FRAMES, 1, 1), 0, 4) > 0
    live = power[:, :, None, None] & kept_pair & (inband | extra) | (gap == 0)[:, :, None, None]
    return live.astype(jnp.int32)


def block_scale(key, dims, cuts, least, high):
    def one(axis_at, blocks):
        heights = jax.random.uniform(jax.random.fold_in(jax.random.fold_in(key, 6), axis_at), (blocks,), jnp.float32, least / len(cuts), high / len(cuts))
        return jnp.repeat(jnp.exp(heights), dims[axis_at] // blocks).reshape((-1,) + (1,) * (len(dims) - axis_at - 1))

    level = one(*cuts[0])
    for cut in cuts[1:]:
        level = level * one(*cut)
    return level


def bell_draw(stream_key, dims, deviation, limit, cuts=(), kind=jnp.bfloat16):
    result = jax.random.normal(stream_key, dims, jnp.float32) * deviation
    if len(cuts) > 0:
        result = block_scale(stream_key, dims, cuts, -0.22, 0.18) * result
    return jnp.clip(result, min=-limit, max=limit).astype(kind)


def setup_inputs(seed: int = 0) -> dict:
    streams_of = jax.random.split(jax.random.key(seed), 8)
    return {
        "query_raw": draw_query_raw(jax.random.fold_in(streams_of[7], 71), 0),
        "key_raw": draw_key_raw(jax.random.fold_in(streams_of[7], 71), 0),
        "value_rows": bell_draw(streams_of[2], (CLIPS, TOKENS, WIDTH), 1.0, 6.0, ((0, 16), (1, 16))),
        "out_grad": bell_draw(streams_of[3], (CLIPS, TOKENS, WIDTH), 1.0, 6.0, ((0, 16), (1, 16))),
        "query_gain": draw_query_gain(jax.random.fold_in(streams_of[7], 71), 0),
        "key_gain": draw_key_gain(jax.random.fold_in(streams_of[7], 71), 0),
        "block_mask": draw_block_mask(jax.random.fold_in(streams_of[7], 71), 0),
    }


eps = 1e-06

def head_norm(raw, gain):
    rows = raw.shape[0]
    values = raw.astype(jnp.float32).reshape(rows, HEADS, HEAD_DIM)
    inverse = lax.rsqrt(lax.optimization_barrier(jnp.mean(values * values, axis=2, keepdims=True)) + eps)
    normed = (values * inverse * gain).astype(jnp.bfloat16)
    return (normed, values, inverse)

def norm_back(grad_norm, values, inverse, gain):
    scaled = grad_norm * gain
    grad_raw = inverse * scaled - values * inverse ** 3 * lax.optimization_barrier(jnp.mean(scaled * values, axis=2, keepdims=True))
    gain_part = lax.optimization_barrier(jnp.sum(grad_norm * values * inverse, axis=(0, 1)))
    return (grad_raw, gain_part)

def rounded(value):
    return lax.optimization_barrier(value.astype(jnp.bfloat16)).astype(jnp.float32)

def clip_pass(query, keys, values, grads, query_gain, key_gain, block_mask):
    q_norm, q_vals, q_inv = head_norm(query, query_gain)
    k_norm, k_vals, k_inv = head_norm(keys, key_gain)
    shape = (FRAMES, FRAME_TOK, HEADS, HEAD_DIM)
    q_full = q_norm.reshape(shape).astype(jnp.float32)
    k_full = k_norm.reshape(shape).astype(jnp.float32)
    v_full = values.reshape(shape).astype(jnp.float32)
    g_full = grads.reshape(shape).astype(jnp.float32)
    scale = HEAD_DIM ** (-0.5)
    offsets = [0]
    for level in range(LEVELS):
        offsets = offsets + [1 << level, -(1 << level)]
    frame_ids = jnp.arange(FRAMES, dtype=jnp.int32)
    scores = []
    for offset in offsets:
        target = frame_ids + offset
        valid = (target >= 0) & (target < FRAMES)
        cells = block_mask[frame_ids, jnp.clip(target, 0, FRAMES - 1)]
        keep = (cells > 0) & valid[:, None, None]
        keep = jnp.repeat(jnp.repeat(keep, BLK, axis=1), BLK, axis=2)
        raw = jnp.einsum('fqhd,fkhd->fhqk', q_full, jnp.roll(k_full, -offset, axis=0)) * scale
        scores.append(jnp.where(keep[:, None], raw, -jnp.inf))
    top = functools.reduce(jnp.maximum, [lax.optimization_barrier(jnp.max(s, axis=3)) for s in scores])
    total = functools.reduce(jnp.add, [lax.optimization_barrier(jnp.sum(jnp.exp(s - top[..., None]), axis=3)) for s in scores])
    lse = top + jnp.log(total)
    probs = [jnp.exp(s - lse[..., None]) for s in scores]
    attn = jnp.zeros(shape, jnp.float32)
    for offset, prob in zip(offsets, probs):
        attn = attn + jnp.einsum('fhqk,fkhd->fqhd', rounded(prob), jnp.roll(v_full, -offset, axis=0))
    attn_b = attn.astype(jnp.bfloat16)
    delta = lax.optimization_barrier(jnp.sum(g_full * attn_b.astype(jnp.float32), axis=3))
    delta = jnp.transpose(delta, (0, 2, 1))
    grad_q = jnp.zeros(shape, jnp.float32)
    grad_k = jnp.zeros(shape, jnp.float32)
    grad_v = jnp.zeros(shape, jnp.float32)
    for offset, prob in zip(offsets, probs):
        key_piece = jnp.roll(k_full, -offset, axis=0)
        value_piece = jnp.roll(v_full, -offset, axis=0)
        dprob = jnp.einsum('fqhd,fkhd->fhqk', g_full, value_piece)
        dscore = rounded(prob * (dprob - delta[..., None]) * scale)
        grad_q = grad_q + jnp.einsum('fhqk,fkhd->fqhd', dscore, key_piece)
        k_term = jnp.einsum('fhqk,fqhd->fkhd', dscore, q_full)
        v_term = jnp.einsum('fhqk,fqhd->fkhd', rounded(prob), g_full)
        if offset == 0:
            grad_k = grad_k + k_term
            grad_v = grad_v + v_term
        else:
            grad_k = grad_k + jnp.roll(rounded(k_term), offset, axis=0)
            grad_v = grad_v + jnp.roll(rounded(v_term), offset, axis=0)
    flat = (TOKENS, HEADS, HEAD_DIM)
    q_raw_grad, q_gain_part = norm_back(grad_q.reshape(flat), q_vals, q_inv, query_gain)
    k_raw_grad, k_gain_part = norm_back(grad_k.reshape(flat), k_vals, k_inv, key_gain)
    wide = (TOKENS, HEADS * HEAD_DIM)
    return (attn_b.reshape(wide), q_raw_grad.reshape(wide).astype(jnp.bfloat16), k_raw_grad.reshape(wide).astype(jnp.bfloat16), grad_v.reshape(wide).astype(jnp.bfloat16), q_gain_part, k_gain_part)

def reference(query_raw, key_raw, value_rows, out_grad, query_gain, key_gain, block_mask):

    def one_clip(items):
        return clip_pass(items[0], items[1], items[2], items[3], query_gain, key_gain, block_mask)
    attn, q_grad, k_grad, v_grad, q_gain_terms, k_gain_terms = lax.map(one_clip, (query_raw, key_raw, value_rows, out_grad))
    return (attn, q_grad, k_grad, v_grad, lax.optimization_barrier(jnp.sum(q_gain_terms, axis=0)) / CLIPS, lax.optimization_barrier(jnp.sum(k_gain_terms, axis=0)) / CLIPS)
```

```python
import jax
import jax.numpy as jnp
from jax import lax
from jax.sharding import PartitionSpec as P

HEADS = 12


eps = 1e-06


def shifted(value, axis, by):
    count = lax.axis_size(axis)
    pairs = [(i, i + by) for i in range(count) if 0 <= i + by < count]
    return lax.ppermute(value, axis, pairs)


def head_norm(raw, gain, heads):
    rows = raw.shape[0]
    values = raw.astype(jnp.float32).reshape(rows, heads, -1)
    inverse = lax.rsqrt(jnp.mean(values * values, axis=2, keepdims=True) + eps)
    normed = (values * inverse * gain).astype(jnp.bfloat16)
    return (normed, values, inverse)


def norm_back(grad_norm, values, inverse, gain):
    scaled = grad_norm * gain
    grad_raw = inverse * scaled - values * inverse**3 * jnp.mean(
        scaled * values, axis=2, keepdims=True
    )
    gain_part = jnp.sum(grad_norm * values * inverse, axis=(0, 1))
    return (grad_raw, gain_part)


def pair_keep(block_mask, here, offset, frames, span):
    target = here + offset
    valid = (target >= 0) & (target < frames)
    row_cells = lax.dynamic_index_in_dim(block_mask, here, 0, keepdims=False)
    cells = lax.dynamic_index_in_dim(row_cells, jnp.clip(target, 0, frames - 1), 0, keepdims=False)
    live = (cells > 0) & valid
    return jnp.repeat(jnp.repeat(live, span, axis=0), span, axis=1)


def on_device(query_raw, key_raw, value_rows, out_grad, query_gain, key_gain, block_mask):
    heads = HEADS
    tokens = query_raw.shape[1]
    width = query_raw.shape[2]
    depth = width // heads
    frames = lax.axis_size("tm")
    levels = frames.bit_length() - 1
    here = lax.axis_index("tm")
    span = tokens // block_mask.shape[2]
    scale = depth ** (-0.5)
    q_norm, q_vals, q_inv = head_norm(query_raw[0], query_gain, heads)
    k_norm, k_vals, k_inv = head_norm(key_raw[0], key_gain, heads)
    k_flat = k_norm.reshape(tokens, width)
    v_flat = value_rows[0]
    offsets = [0]
    for level in range(levels):
        offsets = offsets + [1 << level, -(1 << level)]
    kv_here = jnp.stack([k_flat, v_flat])
    partners = [(k_flat, v_flat)]
    for offset in offsets[1:]:
        got = shifted(kv_here, "tm", -offset)
        partners.append((got[0], got[1]))
    keeps = [pair_keep(block_mask, here, offset, frames, span) for offset in offsets]
    scores = []
    for index in range(len(offsets)):
        key_piece = partners[index][0]
        keep = keeps[index]
        raw = (
            jnp.einsum(
                "qhd,khd->hqk",
                q_norm,
                key_piece.reshape(tokens, heads, depth),
                preferred_element_type=jnp.float32,
            )
            * scale
        )
        scores.append(jnp.where(keep[None], raw, -jnp.inf))
    top = scores[0].max(axis=2)
    for piece in scores[1:]:
        top = jnp.maximum(top, piece.max(axis=2))
    total = jnp.zeros_like(top)
    for piece in scores:
        total = total + jnp.sum(jnp.exp(piece - top[..., None]), axis=2)
    lse = top + jnp.log(total)
    probs = [jnp.exp(piece - lse[..., None]) for piece in scores]
    probs_b = [prob.astype(jnp.bfloat16) for prob in probs]
    attn = jnp.zeros((tokens, heads, depth), jnp.float32)
    for index in range(len(offsets)):
        attn = attn + jnp.einsum(
            "hqk,khd->qhd",
            probs_b[index],
            partners[index][1].reshape(tokens, heads, depth),
            preferred_element_type=jnp.float32,
        )
    attn_b = attn.astype(jnp.bfloat16)
    grad_out = out_grad[0].reshape(tokens, heads, depth)
    delta = jnp.sum(grad_out.astype(jnp.float32) * attn_b.astype(jnp.float32), axis=2).T
    grad_q = jnp.zeros((tokens, heads, depth), jnp.float32)
    grad_k = jnp.zeros((tokens, heads, depth), jnp.float32)
    grad_v = jnp.zeros((tokens, heads, depth), jnp.float32)
    for index, offset in enumerate(offsets):
        key_piece = partners[index][0].reshape(tokens, heads, depth)
        value_piece = partners[index][1].reshape(tokens, heads, depth)
        prob = probs[index]
        prob_b = probs_b[index]
        dprob = jnp.einsum(
            "qhd,khd->hqk", grad_out, value_piece, preferred_element_type=jnp.float32
        )
        dscore = (prob * (dprob - delta[..., None]) * scale).astype(jnp.bfloat16)
        q_term = jnp.einsum("hqk,khd->qhd", dscore, key_piece, preferred_element_type=jnp.float32)
        k_term = jnp.einsum("hqk,qhd->khd", dscore, q_norm, preferred_element_type=jnp.float32)
        v_term = jnp.einsum("hqk,qhd->khd", prob_b, grad_out, preferred_element_type=jnp.float32)
        q_term, k_term, v_term = (q_term, k_term, v_term)
        grad_q = grad_q + q_term
        if offset == 0:
            grad_k = k_term
            grad_v = v_term
        else:
            back = shifted(
                jnp.stack(
                    [
                        k_term.astype(jnp.bfloat16).reshape(tokens, width),
                        v_term.astype(jnp.bfloat16).reshape(tokens, width),
                    ]
                ),
                "tm",
                offset,
            )
            k_back, v_back = back[0], back[1]
            grad_k = grad_k + k_back.astype(jnp.float32).reshape(tokens, heads, depth)
            grad_v = grad_v + v_back.astype(jnp.float32).reshape(tokens, heads, depth)
    q_raw_grad, q_gain_part = norm_back(grad_q, q_vals, q_inv, query_gain)
    k_raw_grad, k_gain_part = norm_back(grad_k, k_vals, k_inv, key_gain)
    q_gain_sum, k_gain_sum = lax.psum((q_gain_part, k_gain_part), ("tm", "dp"))
    clips = lax.axis_size("dp")
    return (
        attn_b.reshape(1, tokens, width),
        q_raw_grad.reshape(1, tokens, width).astype(jnp.bfloat16),
        k_raw_grad.reshape(1, tokens, width).astype(jnp.bfloat16),
        grad_v.reshape(1, tokens, width).astype(jnp.bfloat16),
        q_gain_sum / clips,
        k_gain_sum / clips,
    )


def solution(mesh):
    in_specs = (
        P("dp", "tm", None),
        P("dp", "tm", None),
        P("dp", "tm", None),
        P("dp", "tm", None),
        P(),
        P(),
        P(),
    )
    out_specs = (
        P("dp", "tm", None),
        P("dp", "tm", None),
        P("dp", "tm", None),
        P("dp", "tm", None),
        P(),
        P(),
    )
    return jax.shard_map(
        on_device, mesh=mesh, in_specs=in_specs, out_specs=out_specs, check_vma=False
    )
```

```python
import jax
import jax.numpy as jnp
from jax import lax
from jax.sharding import PartitionSpec as P

HEADS = 12


eps = 1e-06


def shifted(value, axis, by):
    count = lax.axis_size(axis)
    pairs = [(i, i + by) for i in range(count) if 0 <= i + by < count]
    return lax.ppermute(value, axis, pairs)


def tree_sum(value, axis):
    count = lax.axis_size(axis)
    if count & (count - 1):
        return lax.psum(value, axis)
    step = 1
    while step < count:
        pairs = [(i, i ^ step) for i in range(count)]
        value = value + lax.ppermute(value, axis, pairs)
        step *= 2
    return value


def head_norm(raw, gain, heads):
    rows = raw.shape[0]
    values = raw.astype(jnp.float32).reshape(rows, heads, -1)
    inverse = lax.rsqrt(jnp.mean(values * values, axis=2, keepdims=True) + eps)
    normed = (values * inverse * gain).astype(jnp.bfloat16)
    return (normed, values, inverse)


def norm_back(grad_norm, values, inverse, gain):
    scaled = grad_norm * gain
    grad_raw = inverse * scaled - values * inverse**3 * jnp.mean(
        scaled * values, axis=2, keepdims=True
    )
    gain_part = jnp.sum(grad_norm * values * inverse, axis=(0, 1))
    return (grad_raw, gain_part)


def pair_keep(block_mask, here, offset, frames, span):
    target = here + offset
    valid = (target >= 0) & (target < frames)
    row_cells = lax.dynamic_index_in_dim(block_mask, here, 0, keepdims=False)
    cells = lax.dynamic_index_in_dim(row_cells, jnp.clip(target, 0, frames - 1), 0, keepdims=False)
    live = (cells > 0) & valid
    return jnp.repeat(jnp.repeat(live, span, axis=0), span, axis=1)


def on_device(query_raw, key_raw, value_rows, out_grad, query_gain, key_gain, block_mask):
    heads = HEADS
    tokens = query_raw.shape[1]
    width = query_raw.shape[2]
    depth = width // heads
    frames = lax.axis_size("tm")
    levels = frames.bit_length() - 1
    here = lax.axis_index("tm")
    span = tokens // block_mask.shape[2]
    scale = depth ** (-0.5)
    q_norm, q_vals, q_inv = head_norm(query_raw[0], query_gain, heads)
    k_norm, k_vals, k_inv = head_norm(key_raw[0], key_gain, heads)
    k_flat = k_norm.reshape(tokens, width)
    v_flat = value_rows[0]
    offsets = [0]
    for level in range(levels):
        offsets = offsets + [1 << level, -(1 << level)]
    kv_here = jnp.stack([k_flat, v_flat])
    partners = [(k_flat, v_flat)]
    for offset in offsets[1:]:
        got = shifted(kv_here, "tm", -offset)
        partners.append((got[0], got[1]))
    keeps = [pair_keep(block_mask, here, offset, frames, span) for offset in offsets]
    scores = []
    for index in range(len(offsets)):
        key_piece = partners[index][0]
        keep = keeps[index]
        raw = (
            jnp.einsum(
                "qhd,khd->hqk",
                q_norm,
                key_piece.reshape(tokens, heads, depth),
                preferred_element_type=jnp.float32,
            )
            * scale
        )
        scores.append(jnp.where(keep[None], raw, -jnp.inf))
    top = scores[0].max(axis=2)
    for piece in scores[1:]:
        top = jnp.maximum(top, piece.max(axis=2))
    total = jnp.zeros_like(top)
    for piece in scores:
        total = total + jnp.sum(jnp.exp(piece - top[..., None]), axis=2)
    lse = top + jnp.log(total)
    probs = [jnp.exp(piece - lse[..., None]) for piece in scores]
    probs_b = [prob.astype(jnp.bfloat16) for prob in probs]
    attn = jnp.zeros((tokens, heads, depth), jnp.float32)
    for index in range(len(offsets)):
        attn = attn + jnp.einsum(
            "hqk,khd->qhd",
            probs_b[index],
            partners[index][1].reshape(tokens, heads, depth),
            preferred_element_type=jnp.float32,
        )
    attn_b = attn.astype(jnp.bfloat16)
    grad_out = out_grad[0].reshape(tokens, heads, depth)
    delta = jnp.sum(grad_out.astype(jnp.float32) * attn_b.astype(jnp.float32), axis=2).T
    grad_q = jnp.zeros((tokens, heads, depth), jnp.float32)
    grad_k = jnp.zeros((tokens, heads, depth), jnp.float32)
    grad_v = jnp.zeros((tokens, heads, depth), jnp.float32)
    for index, offset in enumerate(offsets):
        key_piece = partners[index][0].reshape(tokens, heads, depth)
        value_piece = partners[index][1].reshape(tokens, heads, depth)
        prob = probs[index]
        prob_b = probs_b[index]
        dprob = jnp.einsum(
            "qhd,khd->hqk", grad_out, value_piece, preferred_element_type=jnp.float32
        )
        dscore = (prob * (dprob - delta[..., None]) * scale).astype(jnp.bfloat16)
        q_term = jnp.einsum("hqk,khd->qhd", dscore, key_piece, preferred_element_type=jnp.float32)
        k_term = jnp.einsum("hqk,qhd->khd", dscore, q_norm, preferred_element_type=jnp.float32)
        v_term = jnp.einsum("hqk,qhd->khd", prob_b, grad_out, preferred_element_type=jnp.float32)
        q_term, k_term, v_term = (q_term, k_term, v_term)
        grad_q = grad_q + q_term
        if offset == 0:
            grad_k = k_term
            grad_v = v_term
        else:
            back = shifted(
                jnp.stack(
                    [
                        k_term.astype(jnp.bfloat16).reshape(tokens, width),
                        v_term.astype(jnp.bfloat16).reshape(tokens, width),
                    ]
                ),
                "tm",
                offset,
            )
            k_back, v_back = back[0], back[1]
            grad_k = grad_k + k_back.astype(jnp.float32).reshape(tokens, heads, depth)
            grad_v = grad_v + v_back.astype(jnp.float32).reshape(tokens, heads, depth)
    q_raw_grad, q_gain_part = norm_back(grad_q, q_vals, q_inv, query_gain)
    k_raw_grad, k_gain_part = norm_back(grad_k, k_vals, k_inv, key_gain)
    gain_sums = tree_sum(tree_sum(jnp.stack([q_gain_part, k_gain_part]), "tm"), "dp")
    q_gain_sum, k_gain_sum = gain_sums[0], gain_sums[1]
    clips = lax.axis_size("dp")
    return (
        attn_b.reshape(1, tokens, width),
        q_raw_grad.reshape(1, tokens, width).astype(jnp.bfloat16),
        k_raw_grad.reshape(1, tokens, width).astype(jnp.bfloat16),
        grad_v.reshape(1, tokens, width).astype(jnp.bfloat16),
        q_gain_sum / clips,
        k_gain_sum / clips,
    )


def solution(mesh):
    in_specs = (
        P("dp", "tm", None),
        P("dp", "tm", None),
        P("dp", "tm", None),
        P("dp", "tm", None),
        P(),
        P(),
        P(),
    )
    out_specs = (
        P("dp", "tm", None),
        P("dp", "tm", None),
        P("dp", "tm", None),
        P("dp", "tm", None),
        P(),
        P(),
    )
    return jax.shard_map(
        on_device, mesh=mesh, in_specs=in_specs, out_specs=out_specs, check_vma=False
    )
```

```python
import jax
import jax.numpy as jnp
from jax import lax
from jax.sharding import PartitionSpec as P

HEADS = 12


eps = 1e-06


def shifted(value, axis, by):
    count = lax.axis_size(axis)
    pairs = [(i, i + by) for i in range(count) if 0 <= i + by < count]
    return lax.ppermute(value, axis, pairs)


def tree_sum(value, axis):
    count = lax.axis_size(axis)
    if count & (count - 1):
        return lax.psum(value, axis)
    step = 1
    while step < count:
        pairs = [(i, i ^ step) for i in range(count)]
        value = value + lax.ppermute(value, axis, pairs)
        step *= 2
    return value


def head_norm(raw, gain, heads):
    rows = raw.shape[0]
    values = raw.astype(jnp.float32).reshape(rows, heads, -1)
    inverse = lax.rsqrt(jnp.mean(values * values, axis=2, keepdims=True) + eps)
    normed = (values * inverse * gain).astype(jnp.bfloat16)
    return (normed, values, inverse)


def norm_back(grad_norm, values, inverse, gain):
    scaled = grad_norm * gain
    grad_raw = inverse * scaled - values * inverse**3 * jnp.mean(
        scaled * values, axis=2, keepdims=True
    )
    gain_part = jnp.sum(grad_norm * values * inverse, axis=(0, 1))
    return (grad_raw, gain_part)


def pair_keep(block_mask, here, offset, frames, span):
    target = here + offset
    valid = (target >= 0) & (target < frames)
    row_cells = lax.dynamic_index_in_dim(block_mask, here, 0, keepdims=False)
    cells = lax.dynamic_index_in_dim(row_cells, jnp.clip(target, 0, frames - 1), 0, keepdims=False)
    live = (cells > 0) & valid
    return jnp.repeat(jnp.repeat(live, span, axis=0), span, axis=1)


GROUPS = 2


def group_pass(q_norm, k_norm, v_rows, grad_out, keeps, offsets, scale, ready, hold):
    tokens, heads, depth = q_norm.shape
    width = heads * depth
    k_flat = k_norm.reshape(tokens, width)
    v_flat = v_rows.reshape(tokens, width)
    kv_here = jnp.stack([k_flat, v_flat])
    if ready is not None:
        kv_here = lax.optimization_barrier((kv_here, ready))[0]
    partners = [(k_flat, v_flat)]
    arrived = []
    for offset in offsets[1:]:
        got = shifted(kv_here, "tm", -offset)
        arrived.append(got)
    if hold is not None:
        arrived = lax.optimization_barrier((arrived, hold))[0]
    for got in arrived:
        partners.append((got[0], got[1]))
    scores = []
    for index in range(len(offsets)):
        key_piece = partners[index][0]
        raw = (
            jnp.einsum(
                "qhd,khd->hqk",
                q_norm,
                key_piece.reshape(tokens, heads, depth),
                preferred_element_type=jnp.float32,
            )
            * scale
        )
        scores.append(jnp.where(keeps[index][None], raw, -jnp.inf))
    top = scores[0].max(axis=2)
    for piece in scores[1:]:
        top = jnp.maximum(top, piece.max(axis=2))
    total = jnp.zeros_like(top)
    for piece in scores:
        total = total + jnp.sum(jnp.exp(piece - top[..., None]), axis=2)
    lse = top + jnp.log(total)
    probs = [jnp.exp(piece - lse[..., None]) for piece in scores]
    probs_b = [prob.astype(jnp.bfloat16) for prob in probs]
    attn = jnp.zeros((tokens, heads, depth), jnp.float32)
    for index in range(len(offsets)):
        attn = attn + jnp.einsum(
            "hqk,khd->qhd",
            probs_b[index],
            partners[index][1].reshape(tokens, heads, depth),
            preferred_element_type=jnp.float32,
        )
    attn_b = attn.astype(jnp.bfloat16)
    delta = jnp.sum(grad_out.astype(jnp.float32) * attn_b.astype(jnp.float32), axis=2).T
    grad_q = jnp.zeros((tokens, heads, depth), jnp.float32)
    grad_k = jnp.zeros((tokens, heads, depth), jnp.float32)
    grad_v = jnp.zeros((tokens, heads, depth), jnp.float32)
    for index, offset in enumerate(offsets):
        key_piece = partners[index][0].reshape(tokens, heads, depth)
        value_piece = partners[index][1].reshape(tokens, heads, depth)
        prob = probs[index]
        prob_b = probs_b[index]
        dprob = jnp.einsum(
            "qhd,khd->hqk", grad_out, value_piece, preferred_element_type=jnp.float32
        )
        dscore = (prob * (dprob - delta[..., None]) * scale).astype(jnp.bfloat16)
        q_term = jnp.einsum("hqk,khd->qhd", dscore, key_piece, preferred_element_type=jnp.float32)
        k_term = jnp.einsum("hqk,qhd->khd", dscore, q_norm, preferred_element_type=jnp.float32)
        v_term = jnp.einsum("hqk,qhd->khd", prob_b, grad_out, preferred_element_type=jnp.float32)
        grad_q = grad_q + q_term
        if offset == 0:
            grad_k = k_term
            grad_v = v_term
        else:
            back = shifted(
                jnp.stack(
                    [
                        k_term.astype(jnp.bfloat16).reshape(tokens, width),
                        v_term.astype(jnp.bfloat16).reshape(tokens, width),
                    ]
                ),
                "tm",
                offset,
            )
            grad_k = grad_k + back[0].astype(jnp.float32).reshape(tokens, heads, depth)
            grad_v = grad_v + back[1].astype(jnp.float32).reshape(tokens, heads, depth)
    return attn_b, grad_q, grad_k, grad_v, arrived


def on_device(query_raw, key_raw, value_rows, out_grad, query_gain, key_gain, block_mask):
    heads = HEADS
    tokens = query_raw.shape[1]
    width = query_raw.shape[2]
    depth = width // heads
    frames = lax.axis_size("tm")
    levels = frames.bit_length() - 1
    here = lax.axis_index("tm")
    span = tokens // block_mask.shape[2]
    scale = depth ** (-0.5)
    q_norm, q_vals, q_inv = head_norm(query_raw[0], query_gain, heads)
    k_norm, k_vals, k_inv = head_norm(key_raw[0], key_gain, heads)
    v_rows = value_rows[0].reshape(tokens, heads, depth)
    grad_out = out_grad[0].reshape(tokens, heads, depth)
    offsets = [0]
    for level in range(levels):
        offsets = offsets + [1 << level, -(1 << level)]
    keeps = [pair_keep(block_mask, here, offset, frames, span) for offset in offsets]
    per = heads // GROUPS
    parts = []
    ready = None
    hold = None
    for group in range(GROUPS):
        cut = slice(group * per, (group + 1) * per)
        result = group_pass(
            q_norm[:, cut], k_norm[:, cut], v_rows[:, cut], grad_out[:, cut],
            keeps, offsets, scale, ready, hold,
        )
        ready = result[4]
        hold = (result[2], result[3])
        parts.append(result[:4])
    attn_b, grad_q, grad_k, grad_v = (
        jnp.concatenate([part[i] for part in parts], axis=1) for i in range(4)
    )
    q_raw_grad, q_gain_part = norm_back(grad_q, q_vals, q_inv, query_gain)
    k_raw_grad, k_gain_part = norm_back(grad_k, k_vals, k_inv, key_gain)
    gain_sums = tree_sum(tree_sum(jnp.stack([q_gain_part, k_gain_part]), "tm"), "dp")
    q_gain_sum, k_gain_sum = gain_sums[0], gain_sums[1]
    clips = lax.axis_size("dp")
    return (
        attn_b.reshape(1, tokens, width),
        q_raw_grad.reshape(1, tokens, width).astype(jnp.bfloat16),
        k_raw_grad.reshape(1, tokens, width).astype(jnp.bfloat16),
        grad_v.reshape(1, tokens, width).astype(jnp.bfloat16),
        q_gain_sum / clips,
        k_gain_sum / clips,
    )


def solution(mesh):
    in_specs = (
        P("dp", "tm", None),
        P("dp", "tm", None),
        P("dp", "tm", None),
        P("dp", "tm", None),
        P(),
        P(),
        P(),
    )
    out_specs = (
        P("dp", "tm", None),
        P("dp", "tm", None),
        P("dp", "tm", None),
        P("dp", "tm", None),
        P(),
        P(),
    )
    return jax.shard_map(
        on_device, mesh=mesh, in_specs=in_specs, out_specs=out_specs, check_vma=False
    )
```

```python
import jax
import jax.numpy as jnp
from jax import lax
from jax.sharding import PartitionSpec as P

HEADS = 12


eps = 1e-06


def shifted(value, axis, by):
    count = lax.axis_size(axis)
    pairs = [(i, i + by) for i in range(count) if 0 <= i + by < count]
    return lax.ppermute(value, axis, pairs)


def tree_sum(value, axis):
    count = lax.axis_size(axis)
    if count & (count - 1):
        return lax.psum(value, axis)
    step = 1
    while step < count:
        pairs = [(i, i ^ step) for i in range(count)]
        value = value + lax.ppermute(value, axis, pairs)
        step *= 2
    return value


def head_norm(raw, gain, heads):
    rows = raw.shape[0]
    values = raw.astype(jnp.float32).reshape(rows, heads, -1)
    inverse = lax.rsqrt(jnp.mean(values * values, axis=2, keepdims=True) + eps)
    normed = (values * inverse * gain).astype(jnp.bfloat16)
    return (normed, values, inverse)


def norm_back(grad_norm, values, inverse, gain):
    scaled = grad_norm * gain
    grad_raw = inverse * scaled - values * inverse**3 * jnp.mean(
        scaled * values, axis=2, keepdims=True
    )
    gain_part = jnp.sum(grad_norm * values * inverse, axis=(0, 1))
    return (grad_raw, gain_part)


def pair_keep(block_mask, here, offset, frames, span):
    target = here + offset
    valid = (target >= 0) & (target < frames)
    row_cells = lax.dynamic_index_in_dim(block_mask, here, 0, keepdims=False)
    cells = lax.dynamic_index_in_dim(row_cells, jnp.clip(target, 0, frames - 1), 0, keepdims=False)
    live = (cells > 0) & valid
    return jnp.repeat(jnp.repeat(live, span, axis=0), span, axis=1)


def on_device(query_raw, key_raw, value_rows, out_grad, query_gain, key_gain, block_mask):
    heads = HEADS
    tokens = query_raw.shape[1]
    width = query_raw.shape[2]
    depth = width // heads
    frames = lax.axis_size("tm")
    levels = frames.bit_length() - 1
    here = lax.axis_index("tm")
    span = tokens // block_mask.shape[2]
    scale = depth ** (-0.5)
    q_norm, q_vals, q_inv = head_norm(query_raw[0], query_gain, heads)
    k_norm, k_vals, k_inv = head_norm(key_raw[0], key_gain, heads)
    k_flat = k_norm.reshape(tokens, width)
    v_flat = value_rows[0]
    offsets = [0]
    for level in range(levels):
        offsets = offsets + [1 << level, -(1 << level)]
    kv_here = jnp.stack([k_flat, v_flat])
    partners = [(k_flat, v_flat)]
    for offset in offsets[1:]:
        got = shifted(kv_here, "tm", -offset)
        partners.append((got[0], got[1]))
    keeps = [pair_keep(block_mask, here, offset, frames, span) for offset in offsets]
    scores = []
    for index in range(len(offsets)):
        key_piece = partners[index][0]
        keep = keeps[index]
        raw = (
            jnp.einsum(
                "qhd,khd->hqk",
                q_norm,
                key_piece.reshape(tokens, heads, depth),
                preferred_element_type=jnp.float32,
            )
            * scale
        )
        scores.append(jnp.where(keep[None], raw, -jnp.inf))
    top = scores[0].max(axis=2)
    for piece in scores[1:]:
        top = jnp.maximum(top, piece.max(axis=2))
    total = jnp.zeros_like(top)
    for piece in scores:
        total = total + jnp.sum(jnp.exp(piece - top[..., None]), axis=2)
    lse = top + jnp.log(total)
    probs = [jnp.exp(piece - lse[..., None]) for piece in scores]
    probs_b = [prob.astype(jnp.bfloat16) for prob in probs]
    attn = jnp.zeros((tokens, heads, depth), jnp.float32)
    for index in range(len(offsets)):
        attn = attn + jnp.einsum(
            "hqk,khd->qhd",
            probs_b[index],
            partners[index][1].reshape(tokens, heads, depth),
            preferred_element_type=jnp.float32,
        )
    attn_b = attn.astype(jnp.bfloat16)
    grad_out = out_grad[0].reshape(tokens, heads, depth)
    delta = jnp.sum(grad_out.astype(jnp.float32) * attn_b.astype(jnp.float32), axis=2).T
    grad_q = jnp.zeros((tokens, heads, depth), jnp.float32)
    grad_k = jnp.zeros((tokens, heads, depth), jnp.float32)
    k_gain_far = jnp.zeros((depth,), jnp.float32)
    backs = []
    grad_v = jnp.zeros((tokens, heads, depth), jnp.float32)
    for index, offset in enumerate(offsets):
        key_piece = partners[index][0].reshape(tokens, heads, depth)
        value_piece = partners[index][1].reshape(tokens, heads, depth)
        prob = probs[index]
        prob_b = probs_b[index]
        dprob = jnp.einsum(
            "qhd,khd->hqk", grad_out, value_piece, preferred_element_type=jnp.float32
        )
        dscore = (prob * (dprob - delta[..., None]) * scale).astype(jnp.bfloat16)
        q_term = jnp.einsum("hqk,khd->qhd", dscore, key_piece, preferred_element_type=jnp.float32)
        k_term = jnp.einsum("hqk,qhd->khd", dscore, q_norm, preferred_element_type=jnp.float32)
        v_term = jnp.einsum("hqk,qhd->khd", prob_b, grad_out, preferred_element_type=jnp.float32)
        q_term, k_term, v_term = (q_term, k_term, v_term)
        grad_q = grad_q + q_term
        if offset == 0:
            grad_k = k_term
            grad_v = v_term
            k_gain_near = jnp.sum(k_term * k_vals * k_inv, axis=(0, 1))
        else:
            k_sent = k_term.astype(jnp.bfloat16)
            k_gain_far = k_gain_far + jnp.sum(
                k_sent.astype(jnp.float32) * key_piece.astype(jnp.float32), axis=(0, 1)
            )
            back = shifted(
                jnp.stack(
                    [
                        k_sent.reshape(tokens, width),
                        v_term.astype(jnp.bfloat16).reshape(tokens, width),
                    ]
                ),
                "tm",
                offset,
            )
            backs.append(back)
    q_raw_grad, q_gain_part = norm_back(grad_q, q_vals, q_inv, query_gain)
    k_gain_part = k_gain_near + k_gain_far / key_gain
    gain_sums = tree_sum(tree_sum(jnp.stack([q_gain_part, k_gain_part]), "tm"), "dp")
    backs, gain_sums = lax.optimization_barrier((backs, gain_sums))
    for back in backs:
        grad_k = grad_k + back[0].astype(jnp.float32).reshape(tokens, heads, depth)
        grad_v = grad_v + back[1].astype(jnp.float32).reshape(tokens, heads, depth)
    k_raw_grad = norm_back(grad_k, k_vals, k_inv, key_gain)[0]
    q_gain_sum, k_gain_sum = gain_sums[0], gain_sums[1]
    clips = lax.axis_size("dp")
    return (
        attn_b.reshape(1, tokens, width),
        q_raw_grad.reshape(1, tokens, width).astype(jnp.bfloat16),
        k_raw_grad.reshape(1, tokens, width).astype(jnp.bfloat16),
        grad_v.reshape(1, tokens, width).astype(jnp.bfloat16),
        q_gain_sum / clips,
        k_gain_sum / clips,
    )


def solution(mesh):
    in_specs = (
        P("dp", "tm", None),
        P("dp", "tm", None),
        P("dp", "tm", None),
        P("dp", "tm", None),
        P(),
        P(),
        P(),
    )
    out_specs = (
        P("dp", "tm", None),
        P("dp", "tm", None),
        P("dp", "tm", None),
        P("dp", "tm", None),
        P(),
        P(),
    )
    return jax.shard_map(
        on_device, mesh=mesh, in_specs=in_specs, out_specs=out_specs, check_vma=False
    )
```

```python
import jax
import jax.numpy as jnp
from jax import lax
from jax.sharding import PartitionSpec as P

HEADS = 12


eps = 1e-06


def shifted(value, axis, by, place):
    count = len(place)
    pairs = [(place[i], place[i + by]) for i in range(count) if 0 <= i + by < count]
    return lax.ppermute(value, axis, pairs)


def frame_places(count):
    if count != 16:
        return list(range(count))
    gray = [0, 1, 3, 2]
    return [gray.index(f & 3) * 4 + ((f >> 2) & 1) * 2 + (f >> 3) for f in range(count)]


def tree_sum(value, axis):
    count = lax.axis_size(axis)
    if count & (count - 1):
        return lax.psum(value, axis)
    step = 1
    while step < count:
        pairs = [(i, i ^ step) for i in range(count)]
        value = value + lax.ppermute(value, axis, pairs)
        step *= 2
    return value


def head_norm(raw, gain, heads):
    rows = raw.shape[0]
    values = raw.astype(jnp.float32).reshape(rows, heads, -1)
    inverse = lax.rsqrt(jnp.mean(values * values, axis=2, keepdims=True) + eps)
    normed = (values * inverse * gain).astype(jnp.bfloat16)
    return (normed, values, inverse)


def norm_back(grad_norm, values, inverse, gain):
    scaled = grad_norm * gain
    grad_raw = inverse * scaled - values * inverse**3 * jnp.mean(
        scaled * values, axis=2, keepdims=True
    )
    gain_part = jnp.sum(grad_norm * values * inverse, axis=(0, 1))
    return (grad_raw, gain_part)


def pair_keep(block_mask, here, offset, frames, span):
    target = here + offset
    valid = (target >= 0) & (target < frames)
    row_cells = lax.dynamic_index_in_dim(block_mask, here, 0, keepdims=False)
    cells = lax.dynamic_index_in_dim(row_cells, jnp.clip(target, 0, frames - 1), 0, keepdims=False)
    live = (cells > 0) & valid
    return jnp.repeat(jnp.repeat(live, span, axis=0), span, axis=1)


def on_device(query_raw, key_raw, value_rows, out_grad, query_gain, key_gain, block_mask):
    frames = lax.axis_size("tm")
    clips = lax.axis_size("dp")
    if frames != 16 or clips != 16:
        place = list(range(frames))
        return attend(query_raw, key_raw, value_rows, out_grad, query_gain, key_gain,
                      block_mask, "tm", place, lax.axis_index("tm"))
    place = frame_places(frames)
    there = [(f * clips + c, c * clips + place[f]) for f in range(frames) for c in range(clips)]
    moved = lax.ppermute(
        jnp.stack([query_raw[0], key_raw[0], value_rows[0], out_grad[0]]), ("tm", "dp"), there
    )
    frame_of = [place.index(p) for p in range(frames)]
    here = jnp.array(frame_of, jnp.int32)[lax.axis_index("dp")]
    outs = attend(moved[0:1], moved[1:2], moved[2:3], moved[3:4], query_gain, key_gain,
                  block_mask, "dp", place, here)
    back = [(b, a) for a, b in there]
    home = lax.ppermute(jnp.concatenate(outs[:4]), ("tm", "dp"), back)
    return (home[0:1], home[1:2], home[2:3], home[3:4], outs[4], outs[5])


def attend(query_raw, key_raw, value_rows, out_grad, query_gain, key_gain, block_mask,
           axis, place, here):
    heads = HEADS
    tokens = query_raw.shape[1]
    width = query_raw.shape[2]
    depth = width // heads
    frames = len(place)
    levels = frames.bit_length() - 1
    span = tokens // block_mask.shape[2]
    scale = depth ** (-0.5)
    q_norm, q_vals, q_inv = head_norm(query_raw[0], query_gain, heads)
    k_norm, k_vals, k_inv = head_norm(key_raw[0], key_gain, heads)
    k_flat = k_norm.reshape(tokens, width)
    v_flat = value_rows[0]
    offsets = [0]
    for level in range(levels):
        offsets = offsets + [1 << level, -(1 << level)]
    kv_here = jnp.stack([k_flat, v_flat])
    partners = [(k_flat, v_flat)]
    for offset in offsets[1:]:
        got = shifted(kv_here, axis, -offset, place)
        partners.append((got[0], got[1]))
    keeps = [pair_keep(block_mask, here, offset, frames, span) for offset in offsets]
    scores = []
    for index in range(len(offsets)):
        key_piece = partners[index][0]
        keep = keeps[index]
        raw = (
            jnp.einsum(
                "qhd,khd->hqk",
                q_norm,
                key_piece.reshape(tokens, heads, depth),
                preferred_element_type=jnp.float32,
            )
            * scale
        )
        scores.append(jnp.where(keep[None], raw, -jnp.inf))
    top = scores[0].max(axis=2)
    for piece in scores[1:]:
        top = jnp.maximum(top, piece.max(axis=2))
    total = jnp.zeros_like(top)
    for piece in scores:
        total = total + jnp.sum(jnp.exp(piece - top[..., None]), axis=2)
    lse = top + jnp.log(total)
    probs = [jnp.exp(piece - lse[..., None]) for piece in scores]
    probs_b = [prob.astype(jnp.bfloat16) for prob in probs]
    attn = jnp.zeros((tokens, heads, depth), jnp.float32)
    for index in range(len(offsets)):
        attn = attn + jnp.einsum(
            "hqk,khd->qhd",
            probs_b[index],
            partners[index][1].reshape(tokens, heads, depth),
            preferred_element_type=jnp.float32,
        )
    attn_b = attn.astype(jnp.bfloat16)
    grad_out = out_grad[0].reshape(tokens, heads, depth)
    delta = jnp.sum(grad_out.astype(jnp.float32) * attn_b.astype(jnp.float32), axis=2).T
    grad_q = jnp.zeros((tokens, heads, depth), jnp.float32)
    grad_k = jnp.zeros((tokens, heads, depth), jnp.float32)
    grad_v = jnp.zeros((tokens, heads, depth), jnp.float32)
    for index, offset in enumerate(offsets):
        key_piece = partners[index][0].reshape(tokens, heads, depth)
        value_piece = partners[index][1].reshape(tokens, heads, depth)
        prob = probs[index]
        prob_b = probs_b[index]
        dprob = jnp.einsum(
            "qhd,khd->hqk", grad_out, value_piece, preferred_element_type=jnp.float32
        )
        dscore = (prob * (dprob - delta[..., None]) * scale).astype(jnp.bfloat16)
        q_term = jnp.einsum("hqk,khd->qhd", dscore, key_piece, preferred_element_type=jnp.float32)
        k_term = jnp.einsum("hqk,qhd->khd", dscore, q_norm, preferred_element_type=jnp.float32)
        v_term = jnp.einsum("hqk,qhd->khd", prob_b, grad_out, preferred_element_type=jnp.float32)
        q_term, k_term, v_term = (q_term, k_term, v_term)
        grad_q = grad_q + q_term
        if offset == 0:
            grad_k = k_term
            grad_v = v_term
        else:
            back = shifted(
                jnp.stack(
                    [
                        k_term.astype(jnp.bfloat16).reshape(tokens, width),
                        v_term.astype(jnp.bfloat16).reshape(tokens, width),
                    ]
                ),
                axis,
                offset,
                place,
            )
            k_back, v_back = back[0], back[1]
            grad_k = grad_k + k_back.astype(jnp.float32).reshape(tokens, heads, depth)
            grad_v = grad_v + v_back.astype(jnp.float32).reshape(tokens, heads, depth)
    q_raw_grad, q_gain_part = norm_back(grad_q, q_vals, q_inv, query_gain)
    k_raw_grad, k_gain_part = norm_back(grad_k, k_vals, k_inv, key_gain)
    gain_sums = tree_sum(tree_sum(jnp.stack([q_gain_part, k_gain_part]), "tm"), "dp")
    q_gain_sum, k_gain_sum = gain_sums[0], gain_sums[1]
    clips = lax.axis_size("dp")
    return (
        attn_b.reshape(1, tokens, width),
        q_raw_grad.reshape(1, tokens, width).astype(jnp.bfloat16),
        k_raw_grad.reshape(1, tokens, width).astype(jnp.bfloat16),
        grad_v.reshape(1, tokens, width).astype(jnp.bfloat16),
        q_gain_sum / clips,
        k_gain_sum / clips,
    )


def solution(mesh):
    in_specs = (
        P("dp", "tm", None),
        P("dp", "tm", None),
        P("dp", "tm", None),
        P("dp", "tm", None),
        P(),
        P(),
        P(),
    )
    out_specs = (
        P("dp", "tm", None),
        P("dp", "tm", None),
        P("dp", "tm", None),
        P("dp", "tm", None),
        P(),
        P(),
    )
    return jax.shard_map(
        on_device, mesh=mesh, in_specs=in_specs, out_specs=out_specs, check_vma=False
    )
```

```python
import jax
import jax.numpy as jnp
from jax import lax
from jax.sharding import PartitionSpec as P

HEADS = 12


eps = 1e-06


def shifted(value, axis, by, places):
    count = len(places[0])
    pairs = [
        (row[i], row[i + by]) for row in places for i in range(count) if 0 <= i + by < count
    ]
    return lax.ppermute(value, axis, pairs)


def swapped_place(frame, clip):
    tm = (frame // 4) * 4 + (clip % 2) * 2 + frame % 2
    dp = (clip // 4) * 4 + ((clip // 2) % 2) * 2 + (frame // 2) % 2
    return tm * 16 + dp


def tree_sum(value, axis):
    count = lax.axis_size(axis)
    if count & (count - 1):
        return lax.psum(value, axis)
    step = 1
    while step < count:
        pairs = [(i, i ^ step) for i in range(count)]
        value = value + lax.ppermute(value, axis, pairs)
        step *= 2
    return value


def head_norm(raw, gain, heads):
    rows = raw.shape[0]
    values = raw.astype(jnp.float32).reshape(rows, heads, -1)
    inverse = lax.rsqrt(jnp.mean(values * values, axis=2, keepdims=True) + eps)
    normed = (values * inverse * gain).astype(jnp.bfloat16)
    return (normed, values, inverse)


def norm_back(grad_norm, values, inverse, gain):
    scaled = grad_norm * gain
    grad_raw = inverse * scaled - values * inverse**3 * jnp.mean(
        scaled * values, axis=2, keepdims=True
    )
    gain_part = jnp.sum(grad_norm * values * inverse, axis=(0, 1))
    return (grad_raw, gain_part)


def pair_keep(block_mask, here, offset, frames, span):
    target = here + offset
    valid = (target >= 0) & (target < frames)
    row_cells = lax.dynamic_index_in_dim(block_mask, here, 0, keepdims=False)
    cells = lax.dynamic_index_in_dim(row_cells, jnp.clip(target, 0, frames - 1), 0, keepdims=False)
    live = (cells > 0) & valid
    return jnp.repeat(jnp.repeat(live, span, axis=0), span, axis=1)


def on_device(query_raw, key_raw, value_rows, out_grad, query_gain, key_gain, block_mask):
    frames = lax.axis_size("tm")
    clips = lax.axis_size("dp")
    if frames != 16 or clips != 16:
        places = [list(range(frames))]
        return attend(query_raw, key_raw, value_rows, out_grad, query_gain, key_gain,
                      block_mask, "tm", places, lax.axis_index("tm"))
    places = [[swapped_place(f, c) for f in range(frames)] for c in range(clips)]
    there = [(f * clips + c, places[c][f]) for f in range(frames) for c in range(clips)]
    moved = lax.ppermute(
        jnp.stack([query_raw[0], key_raw[0], value_rows[0], out_grad[0]]), ("tm", "dp"), there
    )
    tm_at = lax.axis_index("tm")
    here = (tm_at // 4) * 4 + (lax.axis_index("dp") % 2) * 2 + tm_at % 2
    outs = attend(moved[0:1], moved[1:2], moved[2:3], moved[3:4], query_gain, key_gain,
                  block_mask, ("tm", "dp"), places, here)
    back = [(b, a) for a, b in there]
    result, gains = lax.optimization_barrier((jnp.concatenate(outs[:4]), outs[4:]))
    home = lax.ppermute(result, ("tm", "dp"), back)
    return (home[0:1], home[1:2], home[2:3], home[3:4], gains[0], gains[1])


def attend(query_raw, key_raw, value_rows, out_grad, query_gain, key_gain, block_mask,
           axis, places, here):
    heads = HEADS
    tokens = query_raw.shape[1]
    width = query_raw.shape[2]
    depth = width // heads
    frames = len(places[0])
    levels = frames.bit_length() - 1
    span = tokens // block_mask.shape[2]
    scale = depth ** (-0.5)
    q_norm, q_vals, q_inv = head_norm(query_raw[0], query_gain, heads)
    k_norm, k_vals, k_inv = head_norm(key_raw[0], key_gain, heads)
    k_flat = k_norm.reshape(tokens, width)
    v_flat = value_rows[0]
    offsets = [0]
    for level in range(levels):
        offsets = offsets + [1 << level, -(1 << level)]
    kv_here = jnp.stack([k_flat, v_flat])
    partners = [(k_flat, v_flat)]
    for offset in offsets[1:]:
        got = shifted(kv_here, axis, -offset, places)
        partners.append((got[0], got[1]))
    keeps = [pair_keep(block_mask, here, offset, frames, span) for offset in offsets]
    scores = []
    for index in range(len(offsets)):
        key_piece = partners[index][0]
        keep = keeps[index]
        raw = (
            jnp.einsum(
                "qhd,khd->hqk",
                q_norm,
                key_piece.reshape(tokens, heads, depth),
                preferred_element_type=jnp.float32,
            )
            * scale
        )
        scores.append(jnp.where(keep[None], raw, -jnp.inf))
    top = scores[0].max(axis=2)
    for piece in scores[1:]:
        top = jnp.maximum(top, piece.max(axis=2))
    total = jnp.zeros_like(top)
    for piece in scores:
        total = total + jnp.sum(jnp.exp(piece - top[..., None]), axis=2)
    lse = top + jnp.log(total)
    probs = [jnp.exp(piece - lse[..., None]) for piece in scores]
    probs_b = [prob.astype(jnp.bfloat16) for prob in probs]
    attn = jnp.zeros((tokens, heads, depth), jnp.float32)
    for index in range(len(offsets)):
        attn = attn + jnp.einsum(
            "hqk,khd->qhd",
            probs_b[index],
            partners[index][1].reshape(tokens, heads, depth),
            preferred_element_type=jnp.float32,
        )
    attn_b = attn.astype(jnp.bfloat16)
    grad_out = out_grad[0].reshape(tokens, heads, depth)
    delta = jnp.sum(grad_out.astype(jnp.float32) * attn_b.astype(jnp.float32), axis=2).T
    grad_q = jnp.zeros((tokens, heads, depth), jnp.float32)
    grad_k = jnp.zeros((tokens, heads, depth), jnp.float32)
    grad_v = jnp.zeros((tokens, heads, depth), jnp.float32)
    for index, offset in enumerate(offsets):
        key_piece = partners[index][0].reshape(tokens, heads, depth)
        value_piece = partners[index][1].reshape(tokens, heads, depth)
        prob = probs[index]
        prob_b = probs_b[index]
        dprob = jnp.einsum(
            "qhd,khd->hqk", grad_out, value_piece, preferred_element_type=jnp.float32
        )
        dscore = (prob * (dprob - delta[..., None]) * scale).astype(jnp.bfloat16)
        q_term = jnp.einsum("hqk,khd->qhd", dscore, key_piece, preferred_element_type=jnp.float32)
        k_term = jnp.einsum("hqk,qhd->khd", dscore, q_norm, preferred_element_type=jnp.float32)
        v_term = jnp.einsum("hqk,qhd->khd", prob_b, grad_out, preferred_element_type=jnp.float32)
        q_term, k_term, v_term = (q_term, k_term, v_term)
        grad_q = grad_q + q_term
        if offset == 0:
            grad_k = k_term
            grad_v = v_term
        else:
            back = shifted(
                jnp.stack(
                    [
                        k_term.astype(jnp.bfloat16).reshape(tokens, width),
                        v_term.astype(jnp.bfloat16).reshape(tokens, width),
                    ]
                ),
                axis,
                offset,
                places,
            )
            k_back, v_back = back[0], back[1]
            grad_k = grad_k + k_back.astype(jnp.float32).reshape(tokens, heads, depth)
            grad_v = grad_v + v_back.astype(jnp.float32).reshape(tokens, heads, depth)
    q_raw_grad, q_gain_part = norm_back(grad_q, q_vals, q_inv, query_gain)
    k_raw_grad, k_gain_part = norm_back(grad_k, k_vals, k_inv, key_gain)
    gain_sums = tree_sum(tree_sum(jnp.stack([q_gain_part, k_gain_part]), "tm"), "dp")
    q_gain_sum, k_gain_sum = gain_sums[0], gain_sums[1]
    clips = lax.axis_size("dp")
    return (
        attn_b.reshape(1, tokens, width),
        q_raw_grad.reshape(1, tokens, width).astype(jnp.bfloat16),
        k_raw_grad.reshape(1, tokens, width).astype(jnp.bfloat16),
        grad_v.reshape(1, tokens, width).astype(jnp.bfloat16),
        q_gain_sum / clips,
        k_gain_sum / clips,
    )


def solution(mesh):
    in_specs = (
        P("dp", "tm", None),
        P("dp", "tm", None),
        P("dp", "tm", None),
        P("dp", "tm", None),
        P(),
        P(),
        P(),
    )
    out_specs = (
        P("dp", "tm", None),
        P("dp", "tm", None),
        P("dp", "tm", None),
        P("dp", "tm", None),
        P(),
        P(),
    )
    return jax.shard_map(
        on_device, mesh=mesh, in_specs=in_specs, out_specs=out_specs, check_vma=False
    )
```

```python
import jax
import jax.numpy as jnp
from jax import lax
from jax.sharding import PartitionSpec as P

HEADS = 12


eps = 1e-06


def shifted(value, axis, by, places):
    count = len(places[0])
    pairs = [
        (row[i], row[i + by]) for row in places for i in range(count) if 0 <= i + by < count
    ]
    return lax.ppermute(value, axis, pairs)


def swapped_place(frame, clip):
    tm = (frame // 4) * 4 + (clip % 2) * 2 + frame % 2
    dp = (clip // 4) * 4 + ((clip // 2) % 2) * 2 + (frame // 2) % 2
    return tm * 16 + dp


def tree_sum(value, axis):
    count = lax.axis_size(axis)
    if count & (count - 1):
        return lax.psum(value, axis)
    step = 1
    while step < count:
        pairs = [(i, i ^ step) for i in range(count)]
        value = value + lax.ppermute(value, axis, pairs)
        step *= 2
    return value


def head_norm(raw, gain, heads):
    rows = raw.shape[0]
    values = raw.astype(jnp.float32).reshape(rows, heads, -1)
    inverse = lax.rsqrt(jnp.mean(values * values, axis=2, keepdims=True) + eps)
    normed = (values * inverse * gain).astype(jnp.bfloat16)
    return (normed, values, inverse)


def norm_back(grad_norm, values, inverse, gain):
    scaled = grad_norm * gain
    grad_raw = inverse * scaled - values * inverse**3 * jnp.mean(
        scaled * values, axis=2, keepdims=True
    )
    gain_part = jnp.sum(grad_norm * values * inverse, axis=(0, 1))
    return (grad_raw, gain_part)


def pair_keep(block_mask, here, offset, frames, span):
    target = here + offset
    valid = (target >= 0) & (target < frames)
    row_cells = lax.dynamic_index_in_dim(block_mask, here, 0, keepdims=False)
    cells = lax.dynamic_index_in_dim(row_cells, jnp.clip(target, 0, frames - 1), 0, keepdims=False)
    live = (cells > 0) & valid
    return jnp.repeat(jnp.repeat(live, span, axis=0), span, axis=1)


def on_device(query_raw, key_raw, value_rows, out_grad, query_gain, key_gain, block_mask):
    frames = lax.axis_size("tm")
    clips = lax.axis_size("dp")
    if frames != 16 or clips != 16:
        places = [list(range(frames))]
        outs = attend(query_raw, key_raw, value_rows, out_grad, query_gain, key_gain,
                      block_mask, "tm", places, lax.axis_index("tm"))
        gains = tree_sum(tree_sum(outs[4], "tm"), "dp") / clips
        return outs[:4] + (gains[0], gains[1])
    places = [[swapped_place(f, c) for f in range(frames)] for c in range(clips)]
    there = [(f * clips + c, places[c][f]) for f in range(frames) for c in range(clips)]
    moved = lax.ppermute(
        jnp.stack([query_raw[0], key_raw[0], value_rows[0], out_grad[0]]), ("tm", "dp"), there
    )
    tm_at = lax.axis_index("tm")
    here = (tm_at // 4) * 4 + (lax.axis_index("dp") % 2) * 2 + tm_at % 2
    outs = attend(moved[0:1], moved[1:2], moved[2:3], moved[3:4], query_gain, key_gain,
                  block_mask, ("tm", "dp"), places, here)
    back = [(b, a) for a, b in there]
    early = lax.ppermute(jnp.concatenate(outs[:2]), ("tm", "dp"), back)
    parts, early = lax.optimization_barrier((outs[4], early))
    gains = tree_sum(tree_sum(parts, "tm"), "dp") / clips
    late, gains = lax.optimization_barrier((jnp.concatenate(outs[2:4]), gains))
    late = lax.ppermute(late, ("tm", "dp"), back)
    return (early[0:1], early[1:2], late[0:1], late[1:2], gains[0], gains[1])


def attend(query_raw, key_raw, value_rows, out_grad, query_gain, key_gain, block_mask,
           axis, places, here):
    heads = HEADS
    tokens = query_raw.shape[1]
    width = query_raw.shape[2]
    depth = width // heads
    frames = len(places[0])
    levels = frames.bit_length() - 1
    span = tokens // block_mask.shape[2]
    scale = depth ** (-0.5)
    q_norm, q_vals, q_inv = head_norm(query_raw[0], query_gain, heads)
    k_norm, k_vals, k_inv = head_norm(key_raw[0], key_gain, heads)
    k_flat = k_norm.reshape(tokens, width)
    v_flat = value_rows[0]
    offsets = [0]
    for level in range(levels):
        offsets = offsets + [1 << level, -(1 << level)]
    kv_here = jnp.stack([k_flat, v_flat])
    partners = [(k_flat, v_flat)]
    for offset in offsets[1:]:
        got = shifted(kv_here, axis, -offset, places)
        partners.append((got[0], got[1]))
    keeps = [pair_keep(block_mask, here, offset, frames, span) for offset in offsets]
    scores = []
    for index in range(len(offsets)):
        key_piece = partners[index][0]
        keep = keeps[index]
        raw = (
            jnp.einsum(
                "qhd,khd->hqk",
                q_norm,
                key_piece.reshape(tokens, heads, depth),
                preferred_element_type=jnp.float32,
            )
            * scale
        )
        scores.append(jnp.where(keep[None], raw, -jnp.inf))
    top = scores[0].max(axis=2)
    for piece in scores[1:]:
        top = jnp.maximum(top, piece.max(axis=2))
    total = jnp.zeros_like(top)
    for piece in scores:
        total = total + jnp.sum(jnp.exp(piece - top[..., None]), axis=2)
    lse = top + jnp.log(total)
    probs = [jnp.exp(piece - lse[..., None]) for piece in scores]
    probs_b = [prob.astype(jnp.bfloat16) for prob in probs]
    attn = jnp.zeros((tokens, heads, depth), jnp.float32)
    for index in range(len(offsets)):
        attn = attn + jnp.einsum(
            "hqk,khd->qhd",
            probs_b[index],
            partners[index][1].reshape(tokens, heads, depth),
            preferred_element_type=jnp.float32,
        )
    attn_b = attn.astype(jnp.bfloat16)
    grad_out = out_grad[0].reshape(tokens, heads, depth)
    delta = jnp.sum(grad_out.astype(jnp.float32) * attn_b.astype(jnp.float32), axis=2).T
    grad_q = jnp.zeros((tokens, heads, depth), jnp.float32)
    grad_k = jnp.zeros((tokens, heads, depth), jnp.float32)
    grad_v = jnp.zeros((tokens, heads, depth), jnp.float32)
    for index, offset in enumerate(offsets):
        key_piece = partners[index][0].reshape(tokens, heads, depth)
        value_piece = partners[index][1].reshape(tokens, heads, depth)
        prob = probs[index]
        prob_b = probs_b[index]
        dprob = jnp.einsum(
            "qhd,khd->hqk", grad_out, value_piece, preferred_element_type=jnp.float32
        )
        dscore = (prob * (dprob - delta[..., None]) * scale).astype(jnp.bfloat16)
        q_term = jnp.einsum("hqk,khd->qhd", dscore, key_piece, preferred_element_type=jnp.float32)
        k_term = jnp.einsum("hqk,qhd->khd", dscore, q_norm, preferred_element_type=jnp.float32)
        v_term = jnp.einsum("hqk,qhd->khd", prob_b, grad_out, preferred_element_type=jnp.float32)
        q_term, k_term, v_term = (q_term, k_term, v_term)
        grad_q = grad_q + q_term
        if offset == 0:
            grad_k = k_term
            grad_v = v_term
        else:
            back = shifted(
                jnp.stack(
                    [
                        k_term.astype(jnp.bfloat16).reshape(tokens, width),
                        v_term.astype(jnp.bfloat16).reshape(tokens, width),
                    ]
                ),
                axis,
                offset,
                places,
            )
            k_back, v_back = back[0], back[1]
            grad_k = grad_k + k_back.astype(jnp.float32).reshape(tokens, heads, depth)
            grad_v = grad_v + v_back.astype(jnp.float32).reshape(tokens, heads, depth)
    q_raw_grad, q_gain_part = norm_back(grad_q, q_vals, q_inv, query_gain)
    k_raw_grad, k_gain_part = norm_back(grad_k, k_vals, k_inv, key_gain)
    gain_parts = jnp.stack([q_gain_part, k_gain_part])
    return (
        attn_b.reshape(1, tokens, width),
        q_raw_grad.reshape(1, tokens, width).astype(jnp.bfloat16),
        k_raw_grad.reshape(1, tokens, width).astype(jnp.bfloat16),
        grad_v.reshape(1, tokens, width).astype(jnp.bfloat16),
        gain_parts,
    )


def solution(mesh):
    in_specs = (
        P("dp", "tm", None),
        P("dp", "tm", None),
        P("dp", "tm", None),
        P("dp", "tm", None),
        P(),
        P(),
        P(),
    )
    out_specs = (
        P("dp", "tm", None),
        P("dp", "tm", None),
        P("dp", "tm", None),
        P("dp", "tm", None),
        P(),
        P(),
    )
    return jax.shard_map(
        on_device, mesh=mesh, in_specs=in_specs, out_specs=out_specs, check_vma=False
    )
```

```python
import jax
import jax.numpy as jnp
from jax import lax
from jax.sharding import PartitionSpec as P

HEADS = 12


eps = 1e-06


def shifted(value, axis, by, places):
    count = len(places[0])
    pairs = [
        (row[i], row[i + by]) for row in places for i in range(count) if 0 <= i + by < count
    ]
    return lax.ppermute(value, axis, pairs)


def swapped_place(frame, clip):
    tm = (frame // 4) * 4 + ((clip // 2) % 2) * 2 + frame % 2
    dp = (clip // 4) * 4 + ((frame // 2) % 2) * 2 + clip % 2
    return tm * 16 + dp


def tree_sum(value, axis):
    count = lax.axis_size(axis)
    if count & (count - 1):
        return lax.psum(value, axis)
    step = 1
    while step < count:
        pairs = [(i, i ^ step) for i in range(count)]
        value = value + lax.ppermute(value, axis, pairs)
        step *= 2
    return value


def head_norm(raw, gain, heads):
    rows = raw.shape[0]
    values = raw.astype(jnp.float32).reshape(rows, heads, -1)
    inverse = lax.rsqrt(jnp.mean(values * values, axis=2, keepdims=True) + eps)
    normed = (values * inverse * gain).astype(jnp.bfloat16)
    return (normed, values, inverse)


def norm_back(grad_norm, values, inverse, gain):
    scaled = grad_norm * gain
    grad_raw = inverse * scaled - values * inverse**3 * jnp.mean(
        scaled * values, axis=2, keepdims=True
    )
    gain_part = jnp.sum(grad_norm * values * inverse, axis=(0, 1))
    return (grad_raw, gain_part)


def pair_keep(block_mask, here, offset, frames, span):
    target = here + offset
    valid = (target >= 0) & (target < frames)
    row_cells = lax.dynamic_index_in_dim(block_mask, here, 0, keepdims=False)
    cells = lax.dynamic_index_in_dim(row_cells, jnp.clip(target, 0, frames - 1), 0, keepdims=False)
    live = (cells > 0) & valid
    return jnp.repeat(jnp.repeat(live, span, axis=0), span, axis=1)


def on_device(query_raw, key_raw, value_rows, out_grad, query_gain, key_gain, block_mask):
    frames = lax.axis_size("tm")
    clips = lax.axis_size("dp")
    if frames != 16 or clips != 16:
        places = [list(range(frames))]
        return attend(query_raw, key_raw, value_rows, out_grad, query_gain, key_gain,
                      block_mask, "tm", places, lax.axis_index("tm"))
    places = [[swapped_place(f, c) for f in range(frames)] for c in range(clips)]
    there = [(f * clips + c, places[c][f]) for f in range(frames) for c in range(clips)]
    moved = lax.ppermute(
        jnp.stack([query_raw[0], key_raw[0], value_rows[0], out_grad[0]]), ("tm", "dp"), there
    )
    tm_at = lax.axis_index("tm")
    here = (tm_at // 4) * 4 + ((lax.axis_index("dp") // 2) % 2) * 2 + tm_at % 2
    outs = attend(moved[0:1], moved[1:2], moved[2:3], moved[3:4], query_gain, key_gain,
                  block_mask, ("tm", "dp"), places, here)
    back = [(b, a) for a, b in there]
    result, gains = lax.optimization_barrier((jnp.concatenate(outs[:4]), outs[4:]))
    home = lax.ppermute(result, ("tm", "dp"), back)
    return (home[0:1], home[1:2], home[2:3], home[3:4], gains[0], gains[1])


def attend(query_raw, key_raw, value_rows, out_grad, query_gain, key_gain, block_mask,
           axis, places, here):
    heads = HEADS
    tokens = query_raw.shape[1]
    width = query_raw.shape[2]
    depth = width // heads
    frames = len(places[0])
    levels = frames.bit_length() - 1
    span = tokens // block_mask.shape[2]
    scale = depth ** (-0.5)
    q_norm, q_vals, q_inv = head_norm(query_raw[0], query_gain, heads)
    k_norm, k_vals, k_inv = head_norm(key_raw[0], key_gain, heads)
    k_flat = k_norm.reshape(tokens, width)
    v_flat = value_rows[0]
    offsets = [0]
    for level in range(levels):
        offsets = offsets + [1 << level, -(1 << level)]
    kv_here = jnp.stack([k_flat, v_flat])
    partners = [(k_flat, v_flat)]
    for offset in offsets[1:]:
        got = shifted(kv_here, axis, -offset, places)
        partners.append((got[0], got[1]))
    keeps = [pair_keep(block_mask, here, offset, frames, span) for offset in offsets]
    scores = []
    for index in range(len(offsets)):
        key_piece = partners[index][0]
        keep = keeps[index]
        raw = (
            jnp.einsum(
                "qhd,khd->hqk",
                q_norm,
                key_piece.reshape(tokens, heads, depth),
                preferred_element_type=jnp.float32,
            )
            * scale
        )
        scores.append(jnp.where(keep[None], raw, -jnp.inf))
    top = scores[0].max(axis=2)
    for piece in scores[1:]:
        top = jnp.maximum(top, piece.max(axis=2))
    total = jnp.zeros_like(top)
    for piece in scores:
        total = total + jnp.sum(jnp.exp(piece - top[..., None]), axis=2)
    lse = top + jnp.log(total)
    probs = [jnp.exp(piece - lse[..., None]) for piece in scores]
    probs_b = [prob.astype(jnp.bfloat16) for prob in probs]
    attn = jnp.zeros((tokens, heads, depth), jnp.float32)
    for index in range(len(offsets)):
        attn = attn + jnp.einsum(
            "hqk,khd->qhd",
            probs_b[index],
            partners[index][1].reshape(tokens, heads, depth),
            preferred_element_type=jnp.float32,
        )
    attn_b = attn.astype(jnp.bfloat16)
    grad_out = out_grad[0].reshape(tokens, heads, depth)
    delta = jnp.sum(grad_out.astype(jnp.float32) * attn_b.astype(jnp.float32), axis=2).T
    grad_q = jnp.zeros((tokens, heads, depth), jnp.float32)
    grad_k = jnp.zeros((tokens, heads, depth), jnp.float32)
    grad_v = jnp.zeros((tokens, heads, depth), jnp.float32)
    for index, offset in enumerate(offsets):
        key_piece = partners[index][0].reshape(tokens, heads, depth)
        value_piece = partners[index][1].reshape(tokens, heads, depth)
        prob = probs[index]
        prob_b = probs_b[index]
        dprob = jnp.einsum(
            "qhd,khd->hqk", grad_out, value_piece, preferred_element_type=jnp.float32
        )
        dscore = (prob * (dprob - delta[..., None]) * scale).astype(jnp.bfloat16)
        q_term = jnp.einsum("hqk,khd->qhd", dscore, key_piece, preferred_element_type=jnp.float32)
        k_term = jnp.einsum("hqk,qhd->khd", dscore, q_norm, preferred_element_type=jnp.float32)
        v_term = jnp.einsum("hqk,qhd->khd", prob_b, grad_out, preferred_element_type=jnp.float32)
        q_term, k_term, v_term = (q_term, k_term, v_term)
        grad_q = grad_q + q_term
        if offset == 0:
            grad_k = k_term
            grad_v = v_term
        else:
            back = shifted(
                jnp.stack(
                    [
                        k_term.astype(jnp.bfloat16).reshape(tokens, width),
                        v_term.astype(jnp.bfloat16).reshape(tokens, width),
                    ]
                ),
                axis,
                offset,
                places,
            )
            k_back, v_back = back[0], back[1]
            grad_k = grad_k + k_back.astype(jnp.float32).reshape(tokens, heads, depth)
            grad_v = grad_v + v_back.astype(jnp.float32).reshape(tokens, heads, depth)
    q_raw_grad, q_gain_part = norm_back(grad_q, q_vals, q_inv, query_gain)
    k_raw_grad, k_gain_part = norm_back(grad_k, k_vals, k_inv, key_gain)
    gain_sums = tree_sum(tree_sum(jnp.stack([q_gain_part, k_gain_part]), "tm"), "dp")
    q_gain_sum, k_gain_sum = gain_sums[0], gain_sums[1]
    clips = lax.axis_size("dp")
    return (
        attn_b.reshape(1, tokens, width),
        q_raw_grad.reshape(1, tokens, width).astype(jnp.bfloat16),
        k_raw_grad.reshape(1, tokens, width).astype(jnp.bfloat16),
        grad_v.reshape(1, tokens, width).astype(jnp.bfloat16),
        q_gain_sum / clips,
        k_gain_sum / clips,
    )


def solution(mesh):
    in_specs = (
        P("dp", "tm", None),
        P("dp", "tm", None),
        P("dp", "tm", None),
        P("dp", "tm", None),
        P(),
        P(),
        P(),
    )
    out_specs = (
        P("dp", "tm", None),
        P("dp", "tm", None),
        P("dp", "tm", None),
        P("dp", "tm", None),
        P(),
        P(),
    )
    return jax.shard_map(
        on_device, mesh=mesh, in_specs=in_specs, out_specs=out_specs, check_vma=False
    )
```

```python
import jax
import jax.numpy as jnp
from jax import lax
from jax.sharding import PartitionSpec as P

HEADS = 12


eps = 1e-06


def shifted(value, axis, by, places):
    count = len(places[0])
    pairs = [
        (row[i], row[i + by]) for row in places for i in range(count) if 0 <= i + by < count
    ]
    return lax.ppermute(value, axis, pairs)


def swapped_place(frame, clip):
    tm = (frame // 4) * 4 + (clip % 2) * 2 + frame % 2
    dp = (clip // 4) * 4 + ((clip // 2) % 2) * 2 + (frame // 2) % 2
    return tm * 16 + dp


def tree_sum(value, axis):
    count = lax.axis_size(axis)
    if count & (count - 1):
        return lax.psum(value, axis)
    step = 1
    while step < count:
        pairs = [(i, i ^ step) for i in range(count)]
        value = value + lax.ppermute(value, axis, pairs)
        step *= 2
    return value


def head_norm(raw, gain, heads):
    rows = raw.shape[0]
    values = raw.astype(jnp.float32).reshape(rows, heads, -1)
    inverse = lax.rsqrt(jnp.mean(values * values, axis=2, keepdims=True) + eps)
    normed = (values * inverse * gain).astype(jnp.bfloat16)
    return (normed, values, inverse)


def norm_back(grad_norm, values, inverse, gain):
    scaled = grad_norm * gain
    grad_raw = inverse * scaled - values * inverse**3 * jnp.mean(
        scaled * values, axis=2, keepdims=True
    )
    gain_part = jnp.sum(grad_norm * values * inverse, axis=(0, 1))
    return (grad_raw, gain_part)


def pair_keep(block_mask, here, offset, frames, span):
    target = here + offset
    valid = (target >= 0) & (target < frames)
    row_cells = lax.dynamic_index_in_dim(block_mask, here, 0, keepdims=False)
    cells = lax.dynamic_index_in_dim(row_cells, jnp.clip(target, 0, frames - 1), 0, keepdims=False)
    live = (cells > 0) & valid
    return jnp.repeat(jnp.repeat(live, span, axis=0), span, axis=1)


def on_device(query_raw, key_raw, value_rows, out_grad, query_gain, key_gain, block_mask):
    frames = lax.axis_size("tm")
    clips = lax.axis_size("dp")
    if frames != 16 or clips != 16:
        places = [list(range(frames))]
        return attend(query_raw, key_raw, value_rows, out_grad, query_gain, key_gain,
                      block_mask, "tm", places, lax.axis_index("tm"))
    places = [[swapped_place(f, c) for f in range(frames)] for c in range(clips)]
    there = [(f * clips + c, places[c][f]) for f in range(frames) for c in range(clips)]
    kv_moved = lax.ppermute(jnp.stack([key_raw[0], value_rows[0]]), ("tm", "dp"), there)
    qg_here, kv_moved = lax.optimization_barrier(
        (jnp.stack([query_raw[0], out_grad[0]]), kv_moved)
    )
    qg_moved = lax.ppermute(qg_here, ("tm", "dp"), there)
    tm_at = lax.axis_index("tm")
    here = (tm_at // 4) * 4 + (lax.axis_index("dp") % 2) * 2 + tm_at % 2
    outs = attend(qg_moved[0:1], kv_moved[0:1], kv_moved[1:2], qg_moved[1:2], query_gain, key_gain,
                  block_mask, ("tm", "dp"), places, here)
    back = [(b, a) for a, b in there]
    result, gains = lax.optimization_barrier((jnp.concatenate(outs[:4]), outs[4:]))
    home = lax.ppermute(result, ("tm", "dp"), back)
    return (home[0:1], home[1:2], home[2:3], home[3:4], gains[0], gains[1])


def attend(query_raw, key_raw, value_rows, out_grad, query_gain, key_gain, block_mask,
           axis, places, here):
    heads = HEADS
    tokens = query_raw.shape[1]
    width = query_raw.shape[2]
    depth = width // heads
    frames = len(places[0])
    levels = frames.bit_length() - 1
    span = tokens // block_mask.shape[2]
    scale = depth ** (-0.5)
    q_norm, q_vals, q_inv = head_norm(query_raw[0], query_gain, heads)
    k_norm, k_vals, k_inv = head_norm(key_raw[0], key_gain, heads)
    k_flat = k_norm.reshape(tokens, width)
    v_flat = value_rows[0]
    offsets = [0]
    for level in range(levels):
        offsets = offsets + [1 << level, -(1 << level)]
    kv_here = jnp.stack([k_flat, v_flat])
    partners = [(k_flat, v_flat)]
    for offset in offsets[1:]:
        got = shifted(kv_here, axis, -offset, places)
        partners.append((got[0], got[1]))
    keeps = [pair_keep(block_mask, here, offset, frames, span) for offset in offsets]
    scores = []
    for index in range(len(offsets)):
        key_piece = partners[index][0]
        keep = keeps[index]
        raw = (
            jnp.einsum(
                "qhd,khd->hqk",
                q_norm,
                key_piece.reshape(tokens, heads, depth),
                preferred_element_type=jnp.float32,
            )
            * scale
        )
        scores.append(jnp.where(keep[None], raw, -jnp.inf))
    top = scores[0].max(axis=2)
    for piece in scores[1:]:
        top = jnp.maximum(top, piece.max(axis=2))
    total = jnp.zeros_like(top)
    for piece in scores:
        total = total + jnp.sum(jnp.exp(piece - top[..., None]), axis=2)
    lse = top + jnp.log(total)
    probs = [jnp.exp(piece - lse[..., None]) for piece in scores]
    probs_b = [prob.astype(jnp.bfloat16) for prob in probs]
    attn = jnp.zeros((tokens, heads, depth), jnp.float32)
    for index in range(len(offsets)):
        attn = attn + jnp.einsum(
            "hqk,khd->qhd",
            probs_b[index],
            partners[index][1].reshape(tokens, heads, depth),
            preferred_element_type=jnp.float32,
        )
    attn_b = attn.astype(jnp.bfloat16)
    grad_out = out_grad[0].reshape(tokens, heads, depth)
    delta = jnp.sum(grad_out.astype(jnp.float32) * attn_b.astype(jnp.float32), axis=2).T
    grad_q = jnp.zeros((tokens, heads, depth), jnp.float32)
    grad_k = jnp.zeros((tokens, heads, depth), jnp.float32)
    grad_v = jnp.zeros((tokens, heads, depth), jnp.float32)
    for index, offset in enumerate(offsets):
        key_piece = partners[index][0].reshape(tokens, heads, depth)
        value_piece = partners[index][1].reshape(tokens, heads, depth)
        prob = probs[index]
        prob_b = probs_b[index]
        dprob = jnp.einsum(
            "qhd,khd->hqk", grad_out, value_piece, preferred_element_type=jnp.float32
        )
        dscore = (prob * (dprob - delta[..., None]) * scale).astype(jnp.bfloat16)
        q_term = jnp.einsum("hqk,khd->qhd", dscore, key_piece, preferred_element_type=jnp.float32)
        k_term = jnp.einsum("hqk,qhd->khd", dscore, q_norm, preferred_element_type=jnp.float32)
        v_term = jnp.einsum("hqk,qhd->khd", prob_b, grad_out, preferred_element_type=jnp.float32)
        q_term, k_term, v_term = (q_term, k_term, v_term)
        grad_q = grad_q + q_term
        if offset == 0:
            grad_k = k_term
            grad_v = v_term
        else:
            back = shifted(
                jnp.stack(
                    [
                        k_term.astype(jnp.bfloat16).reshape(tokens, width),
                        v_term.astype(jnp.bfloat16).reshape(tokens, width),
                    ]
                ),
                axis,
                offset,
                places,
            )
            k_back, v_back = back[0], back[1]
            grad_k = grad_k + k_back.astype(jnp.float32).reshape(tokens, heads, depth)
            grad_v = grad_v + v_back.astype(jnp.float32).reshape(tokens, heads, depth)
    q_raw_grad, q_gain_part = norm_back(grad_q, q_vals, q_inv, query_gain)
    k_raw_grad, k_gain_part = norm_back(grad_k, k_vals, k_inv, key_gain)
    gain_sums = tree_sum(tree_sum(jnp.stack([q_gain_part, k_gain_part]), "tm"), "dp")
    q_gain_sum, k_gain_sum = gain_sums[0], gain_sums[1]
    clips = lax.axis_size("dp")
    return (
        attn_b.reshape(1, tokens, width),
        q_raw_grad.reshape(1, tokens, width).astype(jnp.bfloat16),
        k_raw_grad.reshape(1, tokens, width).astype(jnp.bfloat16),
        grad_v.reshape(1, tokens, width).astype(jnp.bfloat16),
        q_gain_sum / clips,
        k_gain_sum / clips,
    )


def solution(mesh):
    in_specs = (
        P("dp", "tm", None),
        P("dp", "tm", None),
        P("dp", "tm", None),
        P("dp", "tm", None),
        P(),
        P(),
        P(),
    )
    out_specs = (
        P("dp", "tm", None),
        P("dp", "tm", None),
        P("dp", "tm", None),
        P("dp", "tm", None),
        P(),
        P(),
    )
    return jax.shard_map(
        on_device, mesh=mesh, in_specs=in_specs, out_specs=out_specs, check_vma=False
    )
```

```python
import jax
import jax.numpy as jnp
from jax import lax
from jax.sharding import PartitionSpec as P

HEADS = 12


eps = 1e-06


def shifted(value, axis, by, places):
    count = len(places[0])
    pairs = [
        (row[i], row[i + by]) for row in places for i in range(count) if 0 <= i + by < count
    ]
    return lax.ppermute(value, axis, pairs)


def swapped_place(frame, clip):
    tm = (frame // 4) * 4 + (clip % 2) * 2 + frame % 2
    dp = (clip // 4) * 4 + ((clip // 2) % 2) * 2 + (frame // 2) % 2
    return tm * 16 + dp


def tree_sum(value, axis):
    count = lax.axis_size(axis)
    if count & (count - 1):
        return lax.psum(value, axis)
    step = 1
    while step < count:
        pairs = [(i, i ^ step) for i in range(count)]
        value = value + lax.ppermute(value, axis, pairs)
        step *= 2
    return value


def head_norm(raw, gain, heads):
    rows = raw.shape[0]
    values = raw.astype(jnp.float32).reshape(rows, heads, -1)
    inverse = lax.rsqrt(jnp.mean(values * values, axis=2, keepdims=True) + eps)
    normed = (values * inverse * gain).astype(jnp.bfloat16)
    return (normed, values, inverse)


def norm_back(grad_norm, values, inverse, gain):
    scaled = grad_norm * gain
    grad_raw = inverse * scaled - values * inverse**3 * jnp.mean(
        scaled * values, axis=2, keepdims=True
    )
    gain_part = jnp.sum(grad_norm * values * inverse, axis=(0, 1))
    return (grad_raw, gain_part)


def pair_keep(block_mask, here, offset, frames, span):
    target = here + offset
    valid = (target >= 0) & (target < frames)
    row_cells = lax.dynamic_index_in_dim(block_mask, here, 0, keepdims=False)
    cells = lax.dynamic_index_in_dim(row_cells, jnp.clip(target, 0, frames - 1), 0, keepdims=False)
    live = (cells > 0) & valid
    return jnp.repeat(jnp.repeat(live, span, axis=0), span, axis=1)


def on_device(query_raw, key_raw, value_rows, out_grad, query_gain, key_gain, block_mask):
    frames = lax.axis_size("tm")
    clips = lax.axis_size("dp")
    if frames != 16 or clips != 16:
        places = [list(range(frames))]
        return attend(query_raw, key_raw, value_rows, out_grad, query_gain, key_gain,
                      block_mask, "tm", places, lax.axis_index("tm"))
    places = [[swapped_place(f, c) for f in range(frames)] for c in range(clips)]
    there = [(f * clips + c, places[c][f]) for f in range(frames) for c in range(clips)]
    moved = lax.ppermute(
        jnp.stack([query_raw[0], key_raw[0], value_rows[0], out_grad[0]]), ("tm", "dp"), there
    )
    tm_at = lax.axis_index("tm")
    here = (tm_at // 4) * 4 + (lax.axis_index("dp") % 2) * 2 + tm_at % 2
    outs = attend(moved[0:1], moved[1:2], moved[2:3], moved[3:4], query_gain, key_gain,
                  block_mask, ("tm", "dp"), places, here)
    back = [(b, a) for a, b in there]
    result, gains = lax.optimization_barrier((jnp.concatenate(outs[:4]), outs[4:]))
    home = lax.ppermute(result, ("tm", "dp"), back)
    return (home[0:1], home[1:2], home[2:3], home[3:4], gains[0], gains[1])


def attend(query_raw, key_raw, value_rows, out_grad, query_gain, key_gain, block_mask,
           axis, places, here):
    heads = HEADS
    tokens = query_raw.shape[1]
    width = query_raw.shape[2]
    depth = width // heads
    frames = len(places[0])
    levels = frames.bit_length() - 1
    span = tokens // block_mask.shape[2]
    scale = depth ** (-0.5)
    q_norm, q_vals, q_inv = head_norm(query_raw[0], query_gain, heads)
    k_norm, k_vals, k_inv = head_norm(key_raw[0], key_gain, heads)
    k_flat = k_norm.reshape(tokens, width)
    v_flat = value_rows[0]
    offsets = [0]
    for level in reversed(range(levels)):
        offsets = offsets + [1 << level, -(1 << level)]
    if levels >= 2:
        offsets = offsets[:-4] + offsets[-2:] + offsets[-4:-2]
    kv_here = jnp.stack([k_flat, v_flat])
    partners = [(k_flat, v_flat)]
    for offset in offsets[1:]:
        got = shifted(kv_here, axis, -offset, places)
        partners.append((got[0], got[1]))
    keeps = [pair_keep(block_mask, here, offset, frames, span) for offset in offsets]
    scores = []
    for index in range(len(offsets)):
        key_piece = partners[index][0]
        keep = keeps[index]
        raw = (
            jnp.einsum(
                "qhd,khd->hqk",
                q_norm,
                key_piece.reshape(tokens, heads, depth),
                preferred_element_type=jnp.float32,
            )
            * scale
        )
        scores.append(jnp.where(keep[None], raw, -jnp.inf))
    top = scores[0].max(axis=2)
    for piece in scores[1:]:
        top = jnp.maximum(top, piece.max(axis=2))
    total = jnp.zeros_like(top)
    for piece in scores:
        total = total + jnp.sum(jnp.exp(piece - top[..., None]), axis=2)
    lse = top + jnp.log(total)
    probs = [jnp.exp(piece - lse[..., None]) for piece in scores]
    probs_b = [prob.astype(jnp.bfloat16) for prob in probs]
    attn = jnp.zeros((tokens, heads, depth), jnp.float32)
    for index in range(len(offsets)):
        attn = attn + jnp.einsum(
            "hqk,khd->qhd",
            probs_b[index],
            partners[index][1].reshape(tokens, heads, depth),
            preferred_element_type=jnp.float32,
        )
    attn_b = attn.astype(jnp.bfloat16)
    grad_out = out_grad[0].reshape(tokens, heads, depth)
    delta = jnp.sum(grad_out.astype(jnp.float32) * attn_b.astype(jnp.float32), axis=2).T
    grad_q = jnp.zeros((tokens, heads, depth), jnp.float32)
    grad_k = jnp.zeros((tokens, heads, depth), jnp.float32)
    grad_v = jnp.zeros((tokens, heads, depth), jnp.float32)
    for index, offset in enumerate(offsets):
        key_piece = partners[index][0].reshape(tokens, heads, depth)
        value_piece = partners[index][1].reshape(tokens, heads, depth)
        prob = probs[index]
        prob_b = probs_b[index]
        dprob = jnp.einsum(
            "qhd,khd->hqk", grad_out, value_piece, preferred_element_type=jnp.float32
        )
        dscore = (prob * (dprob - delta[..., None]) * scale).astype(jnp.bfloat16)
        q_term = jnp.einsum("hqk,khd->qhd", dscore, key_piece, preferred_element_type=jnp.float32)
        k_term = jnp.einsum("hqk,qhd->khd", dscore, q_norm, preferred_element_type=jnp.float32)
        v_term = jnp.einsum("hqk,qhd->khd", prob_b, grad_out, preferred_element_type=jnp.float32)
        q_term, k_term, v_term = (q_term, k_term, v_term)
        grad_q = grad_q + q_term
        if offset == 0:
            grad_k = k_term
            grad_v = v_term
        else:
            back = shifted(
                jnp.stack(
                    [
                        k_term.astype(jnp.bfloat16).reshape(tokens, width),
                        v_term.astype(jnp.bfloat16).reshape(tokens, width),
                    ]
                ),
                axis,
                offset,
                places,
            )
            k_back, v_back = back[0], back[1]
            grad_k = grad_k + k_back.astype(jnp.float32).reshape(tokens, heads, depth)
            grad_v = grad_v + v_back.astype(jnp.float32).reshape(tokens, heads, depth)
    q_raw_grad, q_gain_part = norm_back(grad_q, q_vals, q_inv, query_gain)
    k_raw_grad, k_gain_part = norm_back(grad_k, k_vals, k_inv, key_gain)
    gain_sums = tree_sum(tree_sum(jnp.stack([q_gain_part, k_gain_part]), "tm"), "dp")
    q_gain_sum, k_gain_sum = gain_sums[0], gain_sums[1]
    clips = lax.axis_size("dp")
    return (
        attn_b.reshape(1, tokens, width),
        q_raw_grad.reshape(1, tokens, width).astype(jnp.bfloat16),
        k_raw_grad.reshape(1, tokens, width).astype(jnp.bfloat16),
        grad_v.reshape(1, tokens, width).astype(jnp.bfloat16),
        q_gain_sum / clips,
        k_gain_sum / clips,
    )


def solution(mesh):
    in_specs = (
        P("dp", "tm", None),
        P("dp", "tm", None),
        P("dp", "tm", None),
        P("dp", "tm", None),
        P(),
        P(),
        P(),
    )
    out_specs = (
        P("dp", "tm", None),
        P("dp", "tm", None),
        P("dp", "tm", None),
        P("dp", "tm", None),
        P(),
        P(),
    )
    return jax.shard_map(
        on_device, mesh=mesh, in_specs=in_specs, out_specs=out_specs, check_vma=False
    )
```

```python
import jax
import jax.numpy as jnp
from jax import lax
from jax.sharding import PartitionSpec as P

HEADS = 12


eps = 1e-06


def shifted(value, axis, by, places):
    count = len(places[0])
    pairs = [
        (row[i], row[i + by]) for row in places for i in range(count) if 0 <= i + by < count
    ]
    return lax.ppermute(value, axis, pairs)


def swapped_place(frame, clip):
    tm = (frame // 4) * 4 + (clip % 2) * 2 + frame % 2
    dp = (clip // 4) * 4 + ((clip // 2) % 2) * 2 + (frame // 2) % 2
    return tm * 16 + dp


def tree_sum(value, axis):
    count = lax.axis_size(axis)
    if count & (count - 1):
        return lax.psum(value, axis)
    step = 1
    while step < count:
        pairs = [(i, i ^ step) for i in range(count)]
        value = value + lax.ppermute(value, axis, pairs)
        step *= 2
    return value


def head_norm(raw, gain, heads):
    rows = raw.shape[0]
    values = raw.astype(jnp.float32).reshape(rows, heads, -1)
    inverse = lax.rsqrt(jnp.mean(values * values, axis=2, keepdims=True) + eps)
    normed = (values * inverse * gain).astype(jnp.bfloat16)
    return (normed, values, inverse)


def norm_back(grad_norm, values, inverse, gain):
    scaled = grad_norm * gain
    grad_raw = inverse * scaled - values * inverse**3 * jnp.mean(
        scaled * values, axis=2, keepdims=True
    )
    gain_part = jnp.sum(grad_norm * values * inverse, axis=(0, 1))
    return (grad_raw, gain_part)


def pair_keep(block_mask, here, offset, frames, span):
    target = here + offset
    valid = (target >= 0) & (target < frames)
    row_cells = lax.dynamic_index_in_dim(block_mask, here, 0, keepdims=False)
    cells = lax.dynamic_index_in_dim(row_cells, jnp.clip(target, 0, frames - 1), 0, keepdims=False)
    live = (cells > 0) & valid
    return jnp.repeat(jnp.repeat(live, span, axis=0), span, axis=1)


def on_device(query_raw, key_raw, value_rows, out_grad, query_gain, key_gain, block_mask):
    frames = lax.axis_size("tm")
    clips = lax.axis_size("dp")
    if frames != 16 or clips != 16:
        places = [list(range(frames))]
        return attend(query_raw, key_raw, value_rows, out_grad, query_gain, key_gain,
                      block_mask, "tm", places, lax.axis_index("tm"))
    places = [[swapped_place(f, c) for f in range(frames)] for c in range(clips)]
    there = [(f * clips + c, places[c][f]) for f in range(frames) for c in range(clips)]
    moved = lax.ppermute(
        jnp.stack([query_raw[0], key_raw[0], value_rows[0], out_grad[0]]), ("tm", "dp"), there
    )
    tm_at = lax.axis_index("tm")
    here = (tm_at // 4) * 4 + (lax.axis_index("dp") % 2) * 2 + tm_at % 2
    outs = attend(moved[0:1], moved[1:2], moved[2:3], moved[3:4], query_gain, key_gain,
                  block_mask, ("tm", "dp"), places, here)
    back = [(b, a) for a, b in there]
    result, gains = lax.optimization_barrier((jnp.concatenate(outs[:4]), outs[4:]))
    home = lax.ppermute(result, ("tm", "dp"), back)
    return (home[0:1], home[1:2], home[2:3], home[3:4], gains[0], gains[1])


def attend(query_raw, key_raw, value_rows, out_grad, query_gain, key_gain, block_mask,
           axis, places, here):
    heads = HEADS
    tokens = query_raw.shape[1]
    width = query_raw.shape[2]
    depth = width // heads
    frames = len(places[0])
    levels = frames.bit_length() - 1
    span = tokens // block_mask.shape[2]
    scale = depth ** (-0.5)
    q_norm, q_vals, q_inv = head_norm(query_raw[0], query_gain, heads)
    k_norm, k_vals, k_inv = head_norm(key_raw[0], key_gain, heads)
    k_flat = k_norm.reshape(tokens, width)
    v_flat = value_rows[0]
    offsets = [0]
    for level in range(levels):
        offsets = offsets + [1 << level, -(1 << level)]
    kv_here = jnp.stack([k_flat, v_flat])
    partners = [(k_flat, v_flat)]
    for offset in offsets[1:]:
        got = shifted(kv_here, axis, -offset, places)
        partners.append((got[0], got[1]))
    keeps = [pair_keep(block_mask, here, offset, frames, span) for offset in offsets]
    scores = []
    for index in range(len(offsets)):
        key_piece = partners[index][0]
        keep = keeps[index]
        raw = (
            jnp.einsum(
                "qhd,khd->hqk",
                q_norm,
                key_piece.reshape(tokens, heads, depth),
                preferred_element_type=jnp.float32,
            )
            * scale
        )
        scores.append(jnp.where(keep[None], raw, -jnp.inf))
    top = scores[0].max(axis=2)
    for piece in scores[1:]:
        top = jnp.maximum(top, piece.max(axis=2))
    total = jnp.zeros_like(top)
    for piece in scores:
        total = total + jnp.sum(jnp.exp(piece - top[..., None]), axis=2)
    lse = top + jnp.log(total)
    probs = [jnp.exp(piece - lse[..., None]) for piece in scores]
    probs_b = [prob.astype(jnp.bfloat16) for prob in probs]
    attn = jnp.zeros((tokens, heads, depth), jnp.float32)
    for index in range(len(offsets)):
        attn = attn + jnp.einsum(
            "hqk,khd->qhd",
            probs_b[index],
            partners[index][1].reshape(tokens, heads, depth),
            preferred_element_type=jnp.float32,
        )
    attn_b = attn.astype(jnp.bfloat16)
    grad_out = out_grad[0].reshape(tokens, heads, depth)
    delta = jnp.sum(grad_out.astype(jnp.float32) * attn_b.astype(jnp.float32), axis=2).T
    grad_q = jnp.zeros((tokens, heads, depth), jnp.float32)
    grad_k = jnp.zeros((tokens, heads, depth), jnp.float32)
    grad_v = jnp.zeros((tokens, heads, depth), jnp.float32)
    for index, offset in enumerate(offsets):
        key_piece = partners[index][0].reshape(tokens, heads, depth)
        value_piece = partners[index][1].reshape(tokens, heads, depth)
        prob = probs[index]
        prob_b = probs_b[index]
        dprob = jnp.einsum(
            "qhd,khd->hqk", grad_out, value_piece, preferred_element_type=jnp.float32
        )
        dscore = (prob * (dprob - delta[..., None]) * scale).astype(jnp.bfloat16)
        q_term = jnp.einsum("hqk,khd->qhd", dscore, key_piece, preferred_element_type=jnp.float32)
        k_term = jnp.einsum("hqk,qhd->khd", dscore, q_norm, preferred_element_type=jnp.float32)
        v_term = jnp.einsum("hqk,qhd->khd", prob_b, grad_out, preferred_element_type=jnp.float32)
        q_term, k_term, v_term = (q_term, k_term, v_term)
        grad_q = grad_q + q_term
        if offset == 0:
            grad_k = k_term
            grad_v = v_term
        else:
            back = shifted(
                jnp.stack(
                    [
                        k_term.astype(jnp.bfloat16).reshape(tokens, width),
                        v_term.astype(jnp.bfloat16).reshape(tokens, width),
                    ]
                ),
                axis,
                offset,
                places,
            )
            k_back, v_back = back[0], back[1]
            grad_k = grad_k + k_back.astype(jnp.float32).reshape(tokens, heads, depth)
            grad_v = grad_v + v_back.astype(jnp.float32).reshape(tokens, heads, depth)
    q_raw_grad, q_gain_part = norm_back(grad_q, q_vals, q_inv, query_gain)
    k_raw_grad, k_gain_part = norm_back(grad_k, k_vals, k_inv, key_gain)
    gain_sums = tree_sum(tree_sum(jnp.stack([q_gain_part, k_gain_part]), "dp"), "tm")
    q_gain_sum, k_gain_sum = gain_sums[0], gain_sums[1]
    clips = lax.axis_size("dp")
    return (
        attn_b.reshape(1, tokens, width),
        q_raw_grad.reshape(1, tokens, width).astype(jnp.bfloat16),
        k_raw_grad.reshape(1, tokens, width).astype(jnp.bfloat16),
        grad_v.reshape(1, tokens, width).astype(jnp.bfloat16),
        q_gain_sum / clips,
        k_gain_sum / clips,
    )


def solution(mesh):
    in_specs = (
        P("dp", "tm", None),
        P("dp", "tm", None),
        P("dp", "tm", None),
        P("dp", "tm", None),
        P(),
        P(),
        P(),
    )
    out_specs = (
        P("dp", "tm", None),
        P("dp", "tm", None),
        P("dp", "tm", None),
        P("dp", "tm", None),
        P(),
        P(),
    )
    return jax.shard_map(
        on_device, mesh=mesh, in_specs=in_specs, out_specs=out_specs, check_vma=False
    )
```

```python
import jax
import jax.numpy as jnp
from jax import lax
from jax.sharding import PartitionSpec as P

HEADS = 12


eps = 1e-06


def shifted(value, axis, by, places):
    count = len(places[0])
    pairs = [
        (row[i], row[i + by]) for row in places for i in range(count) if 0 <= i + by < count
    ]
    return lax.ppermute(value, axis, pairs)


def swapped_place(frame, clip):
    tm = (frame // 4) * 4 + (clip % 2) * 2 + frame % 2
    dp = (clip // 4) * 4 + ((clip // 2) % 2) * 2 + (frame // 2) % 2
    return tm * 16 + dp


def tree_sum(value, axis):
    count = lax.axis_size(axis)
    if count & (count - 1):
        return lax.psum(value, axis)
    step = 1
    while step < count:
        pairs = [(i, i ^ step) for i in range(count)]
        value = value + lax.ppermute(value, axis, pairs)
        step *= 2
    return value


def head_norm(raw, gain, heads):
    rows = raw.shape[0]
    values = raw.astype(jnp.float32).reshape(rows, heads, -1)
    inverse = lax.rsqrt(jnp.mean(values * values, axis=2, keepdims=True) + eps)
    normed = (values * inverse * gain).astype(jnp.bfloat16)
    return (normed, values, inverse)


def norm_back(grad_norm, values, inverse, gain):
    scaled = grad_norm * gain
    grad_raw = inverse * scaled - values * inverse**3 * jnp.mean(
        scaled * values, axis=2, keepdims=True
    )
    gain_part = jnp.sum(grad_norm * values * inverse, axis=(0, 1))
    return (grad_raw, gain_part)


def pair_keep(block_mask, here, offset, frames, span):
    target = here + offset
    valid = (target >= 0) & (target < frames)
    row_cells = lax.dynamic_index_in_dim(block_mask, here, 0, keepdims=False)
    cells = lax.dynamic_index_in_dim(row_cells, jnp.clip(target, 0, frames - 1), 0, keepdims=False)
    live = (cells > 0) & valid
    return jnp.repeat(jnp.repeat(live, span, axis=0), span, axis=1)


def on_device(query_raw, key_raw, value_rows, out_grad, query_gain, key_gain, block_mask):
    frames = lax.axis_size("tm")
    clips = lax.axis_size("dp")
    if frames != 16 or clips != 16:
        places = [list(range(frames))]
        outs = attend(query_raw, key_raw, value_rows, out_grad, query_gain, key_gain,
                      block_mask, "tm", places, lax.axis_index("tm"))
        gains = tree_sum(tree_sum(outs[4], "tm"), "dp") / clips
        return outs[:4] + (gains[0], gains[1])
    places = [[swapped_place(f, c) for f in range(frames)] for c in range(clips)]
    there = [(f * clips + c, places[c][f]) for f in range(frames) for c in range(clips)]
    moved = lax.ppermute(
        jnp.stack([query_raw[0], key_raw[0], value_rows[0], out_grad[0]]), ("tm", "dp"), there
    )
    tm_at = lax.axis_index("tm")
    here = (tm_at // 4) * 4 + (lax.axis_index("dp") % 2) * 2 + tm_at % 2
    outs = attend(moved[0:1], moved[1:2], moved[2:3], moved[3:4], query_gain, key_gain,
                  block_mask, ("tm", "dp"), places, here)
    back = [(b, a) for a, b in there]
    attn_in = lax.optimization_barrier((outs[0], outs[5]))[0]
    early = lax.ppermute(attn_in, ("tm", "dp"), back)
    parts, early = lax.optimization_barrier((outs[4], early))
    gains = tree_sum(tree_sum(parts, "tm"), "dp") / clips
    late, gains = lax.optimization_barrier((jnp.concatenate(outs[1:4]), gains))
    late = lax.ppermute(late, ("tm", "dp"), back)
    return (early, late[0:1], late[1:2], late[2:3], gains[0], gains[1])


def attend(query_raw, key_raw, value_rows, out_grad, query_gain, key_gain, block_mask,
           axis, places, here):
    heads = HEADS
    tokens = query_raw.shape[1]
    width = query_raw.shape[2]
    depth = width // heads
    frames = len(places[0])
    levels = frames.bit_length() - 1
    span = tokens // block_mask.shape[2]
    scale = depth ** (-0.5)
    q_norm, q_vals, q_inv = head_norm(query_raw[0], query_gain, heads)
    k_norm, k_vals, k_inv = head_norm(key_raw[0], key_gain, heads)
    k_flat = k_norm.reshape(tokens, width)
    v_flat = value_rows[0]
    offsets = [0]
    for level in range(levels):
        offsets = offsets + [1 << level, -(1 << level)]
    kv_here = jnp.stack([k_flat, v_flat])
    partners = [(k_flat, v_flat)]
    for offset in offsets[1:]:
        got = shifted(kv_here, axis, -offset, places)
        partners.append((got[0], got[1]))
    keeps = [pair_keep(block_mask, here, offset, frames, span) for offset in offsets]
    scores = []
    for index in range(len(offsets)):
        key_piece = partners[index][0]
        keep = keeps[index]
        raw = (
            jnp.einsum(
                "qhd,khd->hqk",
                q_norm,
                key_piece.reshape(tokens, heads, depth),
                preferred_element_type=jnp.float32,
            )
            * scale
        )
        scores.append(jnp.where(keep[None], raw, -jnp.inf))
    top = scores[0].max(axis=2)
    for piece in scores[1:]:
        top = jnp.maximum(top, piece.max(axis=2))
    total = jnp.zeros_like(top)
    for piece in scores:
        total = total + jnp.sum(jnp.exp(piece - top[..., None]), axis=2)
    lse = top + jnp.log(total)
    probs = [jnp.exp(piece - lse[..., None]) for piece in scores]
    probs_b = [prob.astype(jnp.bfloat16) for prob in probs]
    attn = jnp.zeros((tokens, heads, depth), jnp.float32)
    for index in range(len(offsets)):
        attn = attn + jnp.einsum(
            "hqk,khd->qhd",
            probs_b[index],
            partners[index][1].reshape(tokens, heads, depth),
            preferred_element_type=jnp.float32,
        )
    attn_b = attn.astype(jnp.bfloat16)
    grad_out = out_grad[0].reshape(tokens, heads, depth)
    delta = jnp.sum(grad_out.astype(jnp.float32) * attn_b.astype(jnp.float32), axis=2).T
    grad_q = jnp.zeros((tokens, heads, depth), jnp.float32)
    grad_k = jnp.zeros((tokens, heads, depth), jnp.float32)
    grad_v = jnp.zeros((tokens, heads, depth), jnp.float32)
    for index, offset in enumerate(offsets):
        key_piece = partners[index][0].reshape(tokens, heads, depth)
        value_piece = partners[index][1].reshape(tokens, heads, depth)
        prob = probs[index]
        prob_b = probs_b[index]
        dprob = jnp.einsum(
            "qhd,khd->hqk", grad_out, value_piece, preferred_element_type=jnp.float32
        )
        dscore = (prob * (dprob - delta[..., None]) * scale).astype(jnp.bfloat16)
        q_term = jnp.einsum("hqk,khd->qhd", dscore, key_piece, preferred_element_type=jnp.float32)
        k_term = jnp.einsum("hqk,qhd->khd", dscore, q_norm, preferred_element_type=jnp.float32)
        v_term = jnp.einsum("hqk,qhd->khd", prob_b, grad_out, preferred_element_type=jnp.float32)
        q_term, k_term, v_term = (q_term, k_term, v_term)
        grad_q = grad_q + q_term
        if offset == 0:
            grad_k = k_term
            grad_v = v_term
        else:
            last_sent = jnp.stack(
                [
                    k_term.astype(jnp.bfloat16).reshape(tokens, width),
                    v_term.astype(jnp.bfloat16).reshape(tokens, width),
                ]
            )
            back = shifted(
                last_sent,
                axis,
                offset,
                places,
            )
            k_back, v_back = back[0], back[1]
            grad_k = grad_k + k_back.astype(jnp.float32).reshape(tokens, heads, depth)
            grad_v = grad_v + v_back.astype(jnp.float32).reshape(tokens, heads, depth)
    q_raw_grad, q_gain_part = norm_back(grad_q, q_vals, q_inv, query_gain)
    k_raw_grad, k_gain_part = norm_back(grad_k, k_vals, k_inv, key_gain)
    return (
        attn_b.reshape(1, tokens, width),
        q_raw_grad.reshape(1, tokens, width).astype(jnp.bfloat16),
        k_raw_grad.reshape(1, tokens, width).astype(jnp.bfloat16),
        grad_v.reshape(1, tokens, width).astype(jnp.bfloat16),
        jnp.stack([q_gain_part, k_gain_part]),
        last_sent,
    )


def solution(mesh):
    in_specs = (
        P("dp", "tm", None),
        P("dp", "tm", None),
        P("dp", "tm", None),
        P("dp", "tm", None),
        P(),
        P(),
        P(),
    )
    out_specs = (
        P("dp", "tm", None),
        P("dp", "tm", None),
        P("dp", "tm", None),
        P("dp", "tm", None),
        P(),
        P(),
    )
    return jax.shard_map(
        on_device, mesh=mesh, in_specs=in_specs, out_specs=out_specs, check_vma=False
    )
```

```python
import jax
import jax.numpy as jnp
from jax import lax
from jax.sharding import PartitionSpec as P

HEADS = 12


eps = 1e-06


def shifted(value, axis, by, places):
    count = len(places[0])
    pairs = [
        (row[i], row[i + by]) for row in places for i in range(count) if 0 <= i + by < count
    ]
    return lax.ppermute(value, axis, pairs)


def swapped_place(frame, clip):
    tm = (frame // 4) * 4 + (clip % 2) * 2 + frame % 2
    dp = (clip // 4) * 4 + ((clip // 2) % 2) * 2 + (frame // 2) % 2
    return tm * 16 + dp


def tree_sum(value, axis):
    count = lax.axis_size(axis)
    if count & (count - 1):
        return lax.psum(value, axis)
    step = 1
    while step < count:
        pairs = [(i, i ^ step) for i in range(count)]
        value = value + lax.ppermute(value, axis, pairs)
        step *= 2
    return value


def rounds_sum(value, rounds):
    for axis, step in rounds:
        count = lax.axis_size(axis)
        pairs = [(i, i ^ step) for i in range(count)]
        value = value + lax.ppermute(value, axis, pairs)
    return value


def head_norm(raw, gain, heads):
    rows = raw.shape[0]
    values = raw.astype(jnp.float32).reshape(rows, heads, -1)
    inverse = lax.rsqrt(jnp.mean(values * values, axis=2, keepdims=True) + eps)
    normed = (values * inverse * gain).astype(jnp.bfloat16)
    return (normed, values, inverse)


def norm_back(grad_norm, values, inverse, gain):
    scaled = grad_norm * gain
    grad_raw = inverse * scaled - values * inverse**3 * jnp.mean(
        scaled * values, axis=2, keepdims=True
    )
    gain_part = jnp.sum(grad_norm * values * inverse, axis=(0, 1))
    return (grad_raw, gain_part)


def pair_keep(block_mask, here, offset, frames, span):
    target = here + offset
    valid = (target >= 0) & (target < frames)
    row_cells = lax.dynamic_index_in_dim(block_mask, here, 0, keepdims=False)
    cells = lax.dynamic_index_in_dim(row_cells, jnp.clip(target, 0, frames - 1), 0, keepdims=False)
    live = (cells > 0) & valid
    return jnp.repeat(jnp.repeat(live, span, axis=0), span, axis=1)


def on_device(query_raw, key_raw, value_rows, out_grad, query_gain, key_gain, block_mask):
    frames = lax.axis_size("tm")
    clips = lax.axis_size("dp")
    if frames != 16 or clips != 16:
        places = [list(range(frames))]
        outs = attend(query_raw, key_raw, value_rows, out_grad, query_gain, key_gain,
                      block_mask, "tm", places, lax.axis_index("tm"))
        gains = tree_sum(tree_sum(outs[4], "tm"), "dp") / clips
        return outs[:4] + (gains[0], gains[1])
    places = [[swapped_place(f, c) for f in range(frames)] for c in range(clips)]
    there = [(f * clips + c, places[c][f]) for f in range(frames) for c in range(clips)]
    moved = lax.ppermute(
        jnp.stack([query_raw[0], key_raw[0], value_rows[0], out_grad[0]]), ("tm", "dp"), there
    )
    tm_at = lax.axis_index("tm")
    here = (tm_at // 4) * 4 + (lax.axis_index("dp") % 2) * 2 + tm_at % 2
    outs = attend(moved[0:1], moved[1:2], moved[2:3], moved[3:4], query_gain, key_gain,
                  block_mask, ("tm", "dp"), places, here)
    back = [(b, a) for a, b in there]
    attn_in = lax.optimization_barrier((outs[0], outs[5]))[0]
    early = lax.ppermute(attn_in, ("tm", "dp"), back)
    late = lax.ppermute(jnp.concatenate(outs[1:4]), ("tm", "dp"), back)
    parts, early = lax.optimization_barrier((outs[4], early))
    rounds = [("tm", 4), ("tm", 8), ("dp", 1), ("dp", 4), ("dp", 8), ("dp", 2), ("tm", 1), ("tm", 2)]
    gains = rounds_sum(parts, rounds) / clips
    return (early, late[0:1], late[1:2], late[2:3], gains[0], gains[1])


def attend(query_raw, key_raw, value_rows, out_grad, query_gain, key_gain, block_mask,
           axis, places, here):
    heads = HEADS
    tokens = query_raw.shape[1]
    width = query_raw.shape[2]
    depth = width // heads
    frames = len(places[0])
    levels = frames.bit_length() - 1
    span = tokens // block_mask.shape[2]
    scale = depth ** (-0.5)
    q_norm, q_vals, q_inv = head_norm(query_raw[0], query_gain, heads)
    k_norm, k_vals, k_inv = head_norm(key_raw[0], key_gain, heads)
    k_flat = k_norm.reshape(tokens, width)
    v_flat = value_rows[0]
    offsets = [0]
    for level in range(levels):
        offsets = offsets + [1 << level, -(1 << level)]
    kv_here = jnp.stack([k_flat, v_flat])
    partners = [(k_flat, v_flat)]
    for offset in offsets[1:]:
        got = shifted(kv_here, axis, -offset, places)
        partners.append((got[0], got[1]))
    keeps = [pair_keep(block_mask, here, offset, frames, span) for offset in offsets]
    scores = []
    for index in range(len(offsets)):
        key_piece = partners[index][0]
        keep = keeps[index]
        raw = (
            jnp.einsum(
                "qhd,khd->hqk",
                q_norm,
                key_piece.reshape(tokens, heads, depth),
                preferred_element_type=jnp.float32,
            )
            * scale
        )
        scores.append(jnp.where(keep[None], raw, -jnp.inf))
    top = scores[0].max(axis=2)
    for piece in scores[1:]:
        top = jnp.maximum(top, piece.max(axis=2))
    total = jnp.zeros_like(top)
    for piece in scores:
        total = total + jnp.sum(jnp.exp(piece - top[..., None]), axis=2)
    lse = top + jnp.log(total)
    probs = [jnp.exp(piece - lse[..., None]) for piece in scores]
    probs_b = [prob.astype(jnp.bfloat16) for prob in probs]
    attn = jnp.zeros((tokens, heads, depth), jnp.float32)
    for index in range(len(offsets)):
        attn = attn + jnp.einsum(
            "hqk,khd->qhd",
            probs_b[index],
            partners[index][1].reshape(tokens, heads, depth),
            preferred_element_type=jnp.float32,
        )
    attn_b = attn.astype(jnp.bfloat16)
    grad_out = out_grad[0].reshape(tokens, heads, depth)
    delta = jnp.sum(grad_out.astype(jnp.float32) * attn_b.astype(jnp.float32), axis=2).T
    grad_q = jnp.zeros((tokens, heads, depth), jnp.float32)
    grad_k = jnp.zeros((tokens, heads, depth), jnp.float32)
    grad_v = jnp.zeros((tokens, heads, depth), jnp.float32)
    for index, offset in enumerate(offsets):
        key_piece = partners[index][0].reshape(tokens, heads, depth)
        value_piece = partners[index][1].reshape(tokens, heads, depth)
        prob = probs[index]
        prob_b = probs_b[index]
        dprob = jnp.einsum(
            "qhd,khd->hqk", grad_out, value_piece, preferred_element_type=jnp.float32
        )
        dscore = (prob * (dprob - delta[..., None]) * scale).astype(jnp.bfloat16)
        q_term = jnp.einsum("hqk,khd->qhd", dscore, key_piece, preferred_element_type=jnp.float32)
        k_term = jnp.einsum("hqk,qhd->khd", dscore, q_norm, preferred_element_type=jnp.float32)
        v_term = jnp.einsum("hqk,qhd->khd", prob_b, grad_out, preferred_element_type=jnp.float32)
        q_term, k_term, v_term = (q_term, k_term, v_term)
        grad_q = grad_q + q_term
        if offset == 0:
            grad_k = k_term
            grad_v = v_term
        else:
            last_sent = jnp.stack(
                [
                    k_term.astype(jnp.bfloat16).reshape(tokens, width),
                    v_term.astype(jnp.bfloat16).reshape(tokens, width),
                ]
            )
            back = shifted(
                last_sent,
                axis,
                offset,
                places,
            )
            k_back, v_back = back[0], back[1]
            grad_k = grad_k + k_back.astype(jnp.float32).reshape(tokens, heads, depth)
            grad_v = grad_v + v_back.astype(jnp.float32).reshape(tokens, heads, depth)
    q_raw_grad, q_gain_part = norm_back(grad_q, q_vals, q_inv, query_gain)
    k_raw_grad, k_gain_part = norm_back(grad_k, k_vals, k_inv, key_gain)
    return (
        attn_b.reshape(1, tokens, width),
        q_raw_grad.reshape(1, tokens, width).astype(jnp.bfloat16),
        k_raw_grad.reshape(1, tokens, width).astype(jnp.bfloat16),
        grad_v.reshape(1, tokens, width).astype(jnp.bfloat16),
        jnp.stack([q_gain_part, k_gain_part]),
        last_sent,
    )


def solution(mesh):
    in_specs = (
        P("dp", "tm", None),
        P("dp", "tm", None),
        P("dp", "tm", None),
        P("dp", "tm", None),
        P(),
        P(),
        P(),
    )
    out_specs = (
        P("dp", "tm", None),
        P("dp", "tm", None),
        P("dp", "tm", None),
        P("dp", "tm", None),
        P(),
        P(),
    )
    return jax.shard_map(
        on_device, mesh=mesh, in_specs=in_specs, out_specs=out_specs, check_vma=False
    )
```

```python
import jax
import jax.numpy as jnp
from jax import lax
from jax.sharding import PartitionSpec as P

HEADS = 12


eps = 1e-06


def shifted(value, axis, by, places):
    count = len(places[0])
    pairs = [
        (row[i], row[i + by]) for row in places for i in range(count) if 0 <= i + by < count
    ]
    return lax.ppermute(value, axis, pairs)


def swapped_place(frame, clip):
    tm = (frame // 4) * 4 + (clip % 2) * 2 + frame % 2
    dp = (clip // 4) * 4 + ((clip // 2) % 2) * 2 + (frame // 2) % 2
    return tm * 16 + dp


def tree_sum(value, axis):
    count = lax.axis_size(axis)
    if count & (count - 1):
        return lax.psum(value, axis)
    step = 1
    while step < count:
        pairs = [(i, i ^ step) for i in range(count)]
        value = value + lax.ppermute(value, axis, pairs)
        step *= 2
    return value


def head_norm(raw, gain, heads):
    rows = raw.shape[0]
    values = raw.astype(jnp.float32).reshape(rows, heads, -1)
    inverse = lax.rsqrt(jnp.mean(values * values, axis=2, keepdims=True) + eps)
    normed = (values * inverse * gain).astype(jnp.bfloat16)
    return (normed, values, inverse)


def norm_back(grad_norm, values, inverse, gain):
    scaled = grad_norm * gain
    grad_raw = inverse * scaled - values * inverse**3 * jnp.mean(
        scaled * values, axis=2, keepdims=True
    )
    gain_part = jnp.sum(grad_norm * values * inverse, axis=(0, 1))
    return (grad_raw, gain_part)


def pair_keep(block_mask, here, offset, frames, span):
    target = here + offset
    valid = (target >= 0) & (target < frames)
    row_cells = lax.dynamic_index_in_dim(block_mask, here, 0, keepdims=False)
    cells = lax.dynamic_index_in_dim(row_cells, jnp.clip(target, 0, frames - 1), 0, keepdims=False)
    live = (cells > 0) & valid
    return jnp.repeat(jnp.repeat(live, span, axis=0), span, axis=1)


def on_device(query_raw, key_raw, value_rows, out_grad, query_gain, key_gain, block_mask):
    frames = lax.axis_size("tm")
    clips = lax.axis_size("dp")
    if frames != 16 or clips != 16:
        places = [list(range(frames))]
        outs = attend(query_raw, key_raw, value_rows, out_grad, query_gain, key_gain,
                      block_mask, "tm", places, lax.axis_index("tm"))
        gains = tree_sum(tree_sum(outs[4], "tm"), "dp") / clips
        return outs[:4] + (gains[0], gains[1])
    places = [[swapped_place(f, c) for f in range(frames)] for c in range(clips)]
    there = [(f * clips + c, places[c][f]) for f in range(frames) for c in range(clips)]
    moved = lax.ppermute(
        jnp.stack([query_raw[0], key_raw[0], value_rows[0], out_grad[0]]), ("tm", "dp"), there
    )
    tm_at = lax.axis_index("tm")
    here = (tm_at // 4) * 4 + (lax.axis_index("dp") % 2) * 2 + tm_at % 2
    outs = attend(moved[0:1], moved[1:2], moved[2:3], moved[3:4], query_gain, key_gain,
                  block_mask, ("tm", "dp"), places, here)
    back = [(b, a) for a, b in there]
    early_in = lax.optimization_barrier((jnp.concatenate(outs[:2]), outs[5]))[0]
    early = lax.ppermute(early_in, ("tm", "dp"), back)
    parts, early = lax.optimization_barrier((outs[4], early))
    gains = tree_sum(tree_sum(parts, "tm"), "dp") / clips
    late, gains = lax.optimization_barrier((jnp.concatenate(outs[2:4]), gains))
    late = lax.ppermute(late, ("tm", "dp"), back)
    return (early[0:1], early[1:2], late[0:1], late[1:2], gains[0], gains[1])


def attend(query_raw, key_raw, value_rows, out_grad, query_gain, key_gain, block_mask,
           axis, places, here):
    heads = HEADS
    tokens = query_raw.shape[1]
    width = query_raw.shape[2]
    depth = width // heads
    frames = len(places[0])
    levels = frames.bit_length() - 1
    span = tokens // block_mask.shape[2]
    scale = depth ** (-0.5)
    q_norm, q_vals, q_inv = head_norm(query_raw[0], query_gain, heads)
    k_norm, k_vals, k_inv = head_norm(key_raw[0], key_gain, heads)
    k_flat = k_norm.reshape(tokens, width)
    v_flat = value_rows[0]
    offsets = [0]
    for level in range(levels):
        offsets = offsets + [1 << level, -(1 << level)]
    kv_here = jnp.stack([k_flat, v_flat])
    partners = [(k_flat, v_flat)]
    for offset in offsets[1:]:
        got = shifted(kv_here, axis, -offset, places)
        partners.append((got[0], got[1]))
    keeps = [pair_keep(block_mask, here, offset, frames, span) for offset in offsets]
    scores = []
    for index in range(len(offsets)):
        key_piece = partners[index][0]
        keep = keeps[index]
        raw = (
            jnp.einsum(
                "qhd,khd->hqk",
                q_norm,
                key_piece.reshape(tokens, heads, depth),
                preferred_element_type=jnp.float32,
            )
            * scale
        )
        scores.append(jnp.where(keep[None], raw, -jnp.inf))
    top = scores[0].max(axis=2)
    for piece in scores[1:]:
        top = jnp.maximum(top, piece.max(axis=2))
    total = jnp.zeros_like(top)
    for piece in scores:
        total = total + jnp.sum(jnp.exp(piece - top[..., None]), axis=2)
    lse = top + jnp.log(total)
    probs = [jnp.exp(piece - lse[..., None]) for piece in scores]
    probs_b = [prob.astype(jnp.bfloat16) for prob in probs]
    attn = jnp.zeros((tokens, heads, depth), jnp.float32)
    for index in range(len(offsets)):
        attn = attn + jnp.einsum(
            "hqk,khd->qhd",
            probs_b[index],
            partners[index][1].reshape(tokens, heads, depth),
            preferred_element_type=jnp.float32,
        )
    attn_b = attn.astype(jnp.bfloat16)
    grad_out = out_grad[0].reshape(tokens, heads, depth)
    delta = jnp.sum(grad_out.astype(jnp.float32) * attn_b.astype(jnp.float32), axis=2).T
    grad_q = jnp.zeros((tokens, heads, depth), jnp.float32)
    grad_k = jnp.zeros((tokens, heads, depth), jnp.float32)
    grad_v = jnp.zeros((tokens, heads, depth), jnp.float32)
    for index, offset in enumerate(offsets):
        key_piece = partners[index][0].reshape(tokens, heads, depth)
        value_piece = partners[index][1].reshape(tokens, heads, depth)
        prob = probs[index]
        prob_b = probs_b[index]
        dprob = jnp.einsum(
            "qhd,khd->hqk", grad_out, value_piece, preferred_element_type=jnp.float32
        )
        dscore = (prob * (dprob - delta[..., None]) * scale).astype(jnp.bfloat16)
        q_term = jnp.einsum("hqk,khd->qhd", dscore, key_piece, preferred_element_type=jnp.float32)
        k_term = jnp.einsum("hqk,qhd->khd", dscore, q_norm, preferred_element_type=jnp.float32)
        v_term = jnp.einsum("hqk,qhd->khd", prob_b, grad_out, preferred_element_type=jnp.float32)
        q_term, k_term, v_term = (q_term, k_term, v_term)
        grad_q = grad_q + q_term
        if offset == 0:
            grad_k = k_term
            grad_v = v_term
        else:
            last_sent = jnp.stack(
                [
                    k_term.astype(jnp.bfloat16).reshape(tokens, width),
                    v_term.astype(jnp.bfloat16).reshape(tokens, width),
                ]
            )
            back = shifted(
                last_sent,
                axis,
                offset,
                places,
            )
            k_back, v_back = back[0], back[1]
            grad_k = grad_k + k_back.astype(jnp.float32).reshape(tokens, heads, depth)
            grad_v = grad_v + v_back.astype(jnp.float32).reshape(tokens, heads, depth)
    q_raw_grad, q_gain_part = norm_back(grad_q, q_vals, q_inv, query_gain)
    k_raw_grad, k_gain_part = norm_back(grad_k, k_vals, k_inv, key_gain)
    return (
        attn_b.reshape(1, tokens, width),
        q_raw_grad.reshape(1, tokens, width).astype(jnp.bfloat16),
        k_raw_grad.reshape(1, tokens, width).astype(jnp.bfloat16),
        grad_v.reshape(1, tokens, width).astype(jnp.bfloat16),
        jnp.stack([q_gain_part, k_gain_part]),
        last_sent,
    )


def solution(mesh):
    in_specs = (
        P("dp", "tm", None),
        P("dp", "tm", None),
        P("dp", "tm", None),
        P("dp", "tm", None),
        P(),
        P(),
        P(),
    )
    out_specs = (
        P("dp", "tm", None),
        P("dp", "tm", None),
        P("dp", "tm", None),
        P("dp", "tm", None),
        P(),
        P(),
    )
    return jax.shard_map(
        on_device, mesh=mesh, in_specs=in_specs, out_specs=out_specs, check_vma=False
    )
```

```python
import jax
import jax.numpy as jnp
from jax import lax
from jax.sharding import PartitionSpec as P

HEADS = 12


eps = 1e-06


def shifted(value, axis, by, places):
    count = len(places[0])
    pairs = [
        (row[i], row[i + by]) for row in places for i in range(count) if 0 <= i + by < count
    ]
    return lax.ppermute(value, axis, pairs)


def swapped_place(frame, clip):
    tm = (frame // 4) * 4 + (clip % 2) * 2 + frame % 2
    dp = (clip // 4) * 4 + ((clip // 2) % 2) * 2 + (frame // 2) % 2
    return tm * 16 + dp


def tree_sum(value, axis):
    count = lax.axis_size(axis)
    if count & (count - 1):
        return lax.psum(value, axis)
    step = 1
    while step < count:
        pairs = [(i, i ^ step) for i in range(count)]
        value = value + lax.ppermute(value, axis, pairs)
        step *= 2
    return value


def head_norm(raw, gain, heads):
    rows = raw.shape[0]
    values = raw.astype(jnp.float32).reshape(rows, heads, -1)
    inverse = lax.rsqrt(jnp.mean(values * values, axis=2, keepdims=True) + eps)
    normed = (values * inverse * gain).astype(jnp.bfloat16)
    return (normed, values, inverse)


def norm_back(grad_norm, values, inverse, gain):
    scaled = grad_norm * gain
    grad_raw = inverse * scaled - values * inverse**3 * jnp.mean(
        scaled * values, axis=2, keepdims=True
    )
    gain_part = jnp.sum(grad_norm * values * inverse, axis=(0, 1))
    return (grad_raw, gain_part)


def pair_keep(block_mask, here, offset, frames, span):
    target = here + offset
    valid = (target >= 0) & (target < frames)
    row_cells = lax.dynamic_index_in_dim(block_mask, here, 0, keepdims=False)
    cells = lax.dynamic_index_in_dim(row_cells, jnp.clip(target, 0, frames - 1), 0, keepdims=False)
    live = (cells > 0) & valid
    return jnp.repeat(jnp.repeat(live, span, axis=0), span, axis=1)


def on_device(query_raw, key_raw, value_rows, out_grad, query_gain, key_gain, block_mask):
    frames = lax.axis_size("tm")
    clips = lax.axis_size("dp")
    if frames != 16 or clips != 16:
        places = [list(range(frames))]
        outs = attend(query_raw, key_raw, value_rows, out_grad, query_gain, key_gain,
                      block_mask, "tm", places, lax.axis_index("tm"))
        gains = tree_sum(tree_sum(outs[4], "tm"), "dp") / clips
        return outs[:4] + (gains[0], gains[1])
    places = [[swapped_place(f, c) for f in range(frames)] for c in range(clips)]
    there = [(f * clips + c, places[c][f]) for f in range(frames) for c in range(clips)]
    moved = lax.ppermute(
        jnp.stack([query_raw[0], key_raw[0], value_rows[0], out_grad[0]]), ("tm", "dp"), there
    )
    tm_at = lax.axis_index("tm")
    here = (tm_at // 4) * 4 + (lax.axis_index("dp") % 2) * 2 + tm_at % 2
    outs = attend(moved[0:1], moved[1:2], moved[2:3], moved[3:4], query_gain, key_gain,
                  block_mask, ("tm", "dp"), places, here)
    back = [(b, a) for a, b in there]
    attn_in = lax.optimization_barrier((outs[0], outs[5]))[0]
    early = lax.ppermute(attn_in, ("tm", "dp"), back)
    parts, early = lax.optimization_barrier((outs[4], early))
    gains = tree_sum(tree_sum(parts, "dp"), "tm") / clips
    late, gains = lax.optimization_barrier((jnp.concatenate(outs[1:4]), gains))
    late = lax.ppermute(late, ("tm", "dp"), back)
    return (early, late[0:1], late[1:2], late[2:3], gains[0], gains[1])


def attend(query_raw, key_raw, value_rows, out_grad, query_gain, key_gain, block_mask,
           axis, places, here):
    heads = HEADS
    tokens = query_raw.shape[1]
    width = query_raw.shape[2]
    depth = width // heads
    frames = len(places[0])
    levels = frames.bit_length() - 1
    span = tokens // block_mask.shape[2]
    scale = depth ** (-0.5)
    q_norm, q_vals, q_inv = head_norm(query_raw[0], query_gain, heads)
    k_norm, k_vals, k_inv = head_norm(key_raw[0], key_gain, heads)
    k_flat = k_norm.reshape(tokens, width)
    v_flat = value_rows[0]
    offsets = [0]
    for level in range(levels):
        offsets = offsets + [1 << level, -(1 << level)]
    kv_here = jnp.stack([k_flat, v_flat])
    partners = [(k_flat, v_flat)]
    for offset in offsets[1:]:
        got = shifted(kv_here, axis, -offset, places)
        partners.append((got[0], got[1]))
    keeps = [pair_keep(block_mask, here, offset, frames, span) for offset in offsets]
    scores = []
    for index in range(len(offsets)):
        key_piece = partners[index][0]
        keep = keeps[index]
        raw = (
            jnp.einsum(
                "qhd,khd->hqk",
                q_norm,
                key_piece.reshape(tokens, heads, depth),
                preferred_element_type=jnp.float32,
            )
            * scale
        )
        scores.append(jnp.where(keep[None], raw, -jnp.inf))
    top = scores[0].max(axis=2)
    for piece in scores[1:]:
        top = jnp.maximum(top, piece.max(axis=2))
    total = jnp.zeros_like(top)
    for piece in scores:
        total = total + jnp.sum(jnp.exp(piece - top[..., None]), axis=2)
    lse = top + jnp.log(total)
    probs = [jnp.exp(piece - lse[..., None]) for piece in scores]
    probs_b = [prob.astype(jnp.bfloat16) for prob in probs]
    attn = jnp.zeros((tokens, heads, depth), jnp.float32)
    for index in range(len(offsets)):
        attn = attn + jnp.einsum(
            "hqk,khd->qhd",
            probs_b[index],
            partners[index][1].reshape(tokens, heads, depth),
            preferred_element_type=jnp.float32,
        )
    attn_b = attn.astype(jnp.bfloat16)
    grad_out = out_grad[0].reshape(tokens, heads, depth)
    delta = jnp.sum(grad_out.astype(jnp.float32) * attn_b.astype(jnp.float32), axis=2).T
    grad_q = jnp.zeros((tokens, heads, depth), jnp.float32)
    grad_k = jnp.zeros((tokens, heads, depth), jnp.float32)
    grad_v = jnp.zeros((tokens, heads, depth), jnp.float32)
    for index, offset in enumerate(offsets):
        key_piece = partners[index][0].reshape(tokens, heads, depth)
        value_piece = partners[index][1].reshape(tokens, heads, depth)
        prob = probs[index]
        prob_b = probs_b[index]
        dprob = jnp.einsum(
            "qhd,khd->hqk", grad_out, value_piece, preferred_element_type=jnp.float32
        )
        dscore = (prob * (dprob - delta[..., None]) * scale).astype(jnp.bfloat16)
        q_term = jnp.einsum("hqk,khd->qhd", dscore, key_piece, preferred_element_type=jnp.float32)
        k_term = jnp.einsum("hqk,qhd->khd", dscore, q_norm, preferred_element_type=jnp.float32)
        v_term = jnp.einsum("hqk,qhd->khd", prob_b, grad_out, preferred_element_type=jnp.float32)
        q_term, k_term, v_term = (q_term, k_term, v_term)
        grad_q = grad_q + q_term
        if offset == 0:
            grad_k = k_term
            grad_v = v_term
        else:
            last_sent = jnp.stack(
                [
                    k_term.astype(jnp.bfloat16).reshape(tokens, width),
                    v_term.astype(jnp.bfloat16).reshape(tokens, width),
                ]
            )
            back = shifted(
                last_sent,
                axis,
                offset,
                places,
            )
            k_back, v_back = back[0], back[1]
            grad_k = grad_k + k_back.astype(jnp.float32).reshape(tokens, heads, depth)
            grad_v = grad_v + v_back.astype(jnp.float32).reshape(tokens, heads, depth)
    q_raw_grad, q_gain_part = norm_back(grad_q, q_vals, q_inv, query_gain)
    k_raw_grad, k_gain_part = norm_back(grad_k, k_vals, k_inv, key_gain)
    return (
        attn_b.reshape(1, tokens, width),
        q_raw_grad.reshape(1, tokens, width).astype(jnp.bfloat16),
        k_raw_grad.reshape(1, tokens, width).astype(jnp.bfloat16),
        grad_v.reshape(1, tokens, width).astype(jnp.bfloat16),
        jnp.stack([q_gain_part, k_gain_part]),
        last_sent,
    )


def solution(mesh):
    in_specs = (
        P("dp", "tm", None),
        P("dp", "tm", None),
        P("dp", "tm", None),
        P("dp", "tm", None),
        P(),
        P(),
        P(),
    )
    out_specs = (
        P("dp", "tm", None),
        P("dp", "tm", None),
        P("dp", "tm", None),
        P("dp", "tm", None),
        P(),
        P(),
    )
    return jax.shard_map(
        on_device, mesh=mesh, in_specs=in_specs, out_specs=out_specs, check_vma=False
    )
```
